256 devices in a mesh: win: 32 (over y, z), grp: 8 (over x, core).
Axes of the slice: x: 4, y: 4, z: 8, core: 2. Of those that a mesh axis runs over, the one named last changes fastest.
Arguments:
- points: bfloat16 [32, 8, 512, 512], P('win', 'grp'), may hold values from -6 to 6
- rank: int32 [32, 8, 512], P('win', 'grp'), may hold values from 0 to 16383, as said below
- counts: int32 [8, 32, 8], replicated, may hold values from 1 to 128, 512 in all within a row
- w_qkv_one: bfloat16 [512, 1536], replicated
- w_out_one: bfloat16 [512, 512], replicated, may hold values from -0.25 to 0.25
- w_up: bfloat16 [512, 2048], replicated, may hold values from -0.25 to 0.25
- w_down: bfloat16 [2048, 512], replicated, may hold values from -0.125 to 0.125
- w_qkv_two: bfloat16 [512, 1536], replicated
- w_out_two: bfloat16 [512, 512], replicated, may hold values from -0.25 to 0.25
Outputs:
- encoded: bfloat16 [32, 8, 512, 512], P('win', 'grp')
The draws below stay inside these ranges and needn't reach their ends.
Inputs may be any that keep to these rules, and one draw needn't show every extreme that they name: Within each of the 8 grp columns, rank over all 32 devices of win is a permutation of 0 to 16383. Each device holds at most 32 points whose rank // 512 is any one owner, and exactly 32 for some owner; each owner receives exactly 32 from some device. For each grp column and owner the 8 counts sum to 512, and the largest is 128.
All inputs are finite; a program needn't handle non-finite values.
Results may differ from the reference program's by a relative error of at most 0.03.
The reference program's roundings to bfloat16 on the way count: a program that leaves them out, or rounds other values in their place, can miss the bound.
Values may be sent and summed in bfloat16 or wider, within the bound.
No kernel may reach another device: no remote copies, remote signals or barrier semaphores. Data moves between devices by JAX's collectives and lax.ppermute only.
A program may use at most 128 MiB of HBM per device.

```python
import math
import jax
import jax.numpy as jnp
import numpy as np
from jax import lax

D = 512
HEADS = 16
HEAD_DIM = 32
FF = 2048
WINDOW_SLOTS = 128
P_DEV = 512
OWNER_WINDOWS = 8
N_WIN = 32
N_GRP = 8


def segment_rank(key):
    base = P_DEV // N_WIN
    keys = jax.random.split(key, 4)
    ids = jnp.arange(N_WIN, dtype=jnp.int32)
    levels = jax.random.randint(keys[0], (N_WIN,), 0, base + 1, dtype=jnp.int32)
    anchor = jax.random.randint(keys[1], (), 0, N_WIN, dtype=jnp.int32)
    levels = jnp.where(ids == anchor, base, levels)
    levels = jnp.where(ids == (anchor - 1) % N_WIN, 0, levels)
    steps_diff = levels - jnp.roll(levels, 1)
    lag = (ids[None, :] - ids[:, None]) % N_WIN
    matrix = base + steps_diff[lag]
    row_end = jnp.cumsum(matrix, axis=1)
    row_start = row_end - matrix
    col_start = jnp.cumsum(matrix, axis=0) - matrix
    owner_perm = jax.vmap(lambda sub_key: jax.random.permutation(sub_key, P_DEV))(jax.random.split(keys[2], N_WIN))
    local_perm = jax.vmap(lambda sub_key: jax.random.permutation(sub_key, P_DEV))(jax.random.split(keys[3], N_WIN))
    slot_ids = jnp.arange(P_DEV, dtype=jnp.int32)

    def source_rank(source, row_ends, row_starts, shuffle):
        owner_of = jnp.sum((row_ends[None, :] <= slot_ids[:, None]).astype(jnp.int32), axis=1)
        inner = slot_ids - row_starts[owner_of]
        pre_position = col_start[source, owner_of] + inner
        position = owner_perm[owner_of, pre_position]
        ranks_pre = owner_of * P_DEV + position
        return ranks_pre[shuffle]
    return jax.vmap(source_rank)(ids, row_end, row_start, local_perm).astype(jnp.int32)


def draw_rank(key, part):
    seg_keys = jax.random.split(jax.random.fold_in(key, 5), N_GRP)
    ranks = jax.vmap(segment_rank)(seg_keys)
    return jnp.transpose(ranks, (1, 0, 2)).astype(jnp.int32)


def qkv_table(key):
    table = jax.random.normal(key, (D, 3, HEADS, HEAD_DIM), jnp.float32) * D ** (-0.5)
    return table.reshape(D, 3 * D).astype(jnp.bfloat16)


def draw_w_qkv_one(key, part):
    return qkv_table(jax.random.fold_in(key, 11))


def draw_w_qkv_two(key, part):
    return qkv_table(jax.random.fold_in(key, 23))


def level_of(stream_key, shape, shards, smallest, largest):
    def one(dim, parts):
        steps = jax.random.uniform(jax.random.fold_in(jax.random.fold_in(stream_key, 6), dim), (parts,), jnp.float32, smallest / len(shards), largest / len(shards))
        return jnp.repeat(jnp.exp(steps), shape[dim] // parts).reshape((-1,) + (1,) * (len(shape) - dim - 1))

    factor_of = one(*shards[0])
    for cut in shards[1:]:
        factor_of = factor_of * one(*cut)
    return factor_of


def split_up(number_of, total, limit, skew):
    weights = [(1 << 20) // math.isqrt(standing ** skew) + 1 for standing in range(2, number_of + 1)]
    rest, holding = total - limit - (number_of - 1), [1] * (number_of - 1)
    while rest > 0:
        movable = [i for i in range(number_of - 1) if holding[i] < limit]
        pool, left = sum([weights[i] for i in movable]), rest
        for i in movable:
            addition = min(limit - holding[i], max(1, left * weights[i] // pool), rest)
            holding[i] = holding[i] + addition
            rest = rest - addition
    return np.array([limit] + holding)


def ragged_sizes(key, number_of, total, most, lean):
    if number_of == 2:
        one = jax.random.randint(key, (), max(1, total - most), min(most, total - 1) + 1)
        return jnp.stack([one, total - one])
    lengths = jnp.asarray(split_up(number_of, total, most, lean), jnp.int32)
    pairs = (number_of - 1) // 2
    donor, sink = lengths[1:1 + 2 * pairs:2], lengths[2:2 + 2 * pairs:2]
    margin = jnp.minimum(donor - 1, most - sink)
    moved = jax.random.randint(jax.random.fold_in(key, 1), (pairs,), 0, 1 << 20) % (margin + 1)
    lengths = lengths.at[1:1 + 2 * pairs:2].set(donor - moved).at[2:2 + 2 * pairs:2].set(sink + moved)
    return lengths[jax.random.permutation(jax.random.fold_in(key, 2), number_of)]


def bell_draw(key, shape, deviation, bound, cuts=(), kind=jnp.bfloat16):
    drawn = jax.random.normal(key, shape, jnp.float32) * deviation
    if len(cuts) > 0:
        drawn = level_of(key, shape, cuts, -0.22, 0.18) * drawn
    return jnp.clip(drawn, min=-bound, max=bound).astype(kind)


def setup_inputs(seed: int = 0) -> dict:
    splits = jax.random.split(jax.random.key(seed), 10)
    points = bell_draw(splits[0], (N_WIN, N_GRP, P_DEV, D), 1.0, 6.0, ((0, 32), (1, 8)))
    rank = draw_rank(jax.random.fold_in(splits[9], 71), 0)
    counts = jax.vmap(lambda own: ragged_sizes(own, OWNER_WINDOWS, P_DEV, WINDOW_SLOTS, 2))(jax.random.split(splits[2], N_GRP * N_WIN)).reshape((N_GRP, N_WIN, OWNER_WINDOWS)).astype(jnp.int32)
    w_qkv_one = draw_w_qkv_one(jax.random.fold_in(splits[9], 71), 0)
    w_out_one = bell_draw(splits[4], (D, D), D ** -0.5, 0.25)
    w_up = bell_draw(splits[5], (D, FF), D ** -0.5, 0.25)
    w_down = bell_draw(splits[6], (FF, D), FF ** -0.5, 0.125)
    w_qkv_two = draw_w_qkv_two(jax.random.fold_in(splits[9], 71), 0)
    w_out_two = bell_draw(splits[8], (D, D), D ** -0.5, 0.25)
    return dict(points=points, rank=rank, counts=counts, w_qkv_one=w_qkv_one, w_out_one=w_out_one, w_up=w_up, w_down=w_down, w_qkv_two=w_qkv_two, w_out_two=w_out_two)


EPSILON = 1e-05
MASKED = -1e+30

def normalize(row_data):
    values = row_data.astype(jnp.float32)
    center = values - lax.optimization_barrier(jnp.mean(values, axis=-1, keepdims=True))
    spread = lax.optimization_barrier(jnp.mean(center * center, axis=-1, keepdims=True))
    return (center * lax.rsqrt(spread + EPSILON)).astype(jnp.bfloat16)

def block_attention(row_data, valid, w_qkv, w_out):
    block_count, width_len, model_dim = row_data.shape
    heads_count = model_dim // HEAD_DIM
    flat_rows = row_data.reshape(block_count * width_len, model_dim)
    packed = jnp.dot(normalize(flat_rows), w_qkv, preferred_element_type=jnp.float32).astype(jnp.bfloat16)
    split_heads = packed.reshape(block_count, width_len, 3, heads_count, HEAD_DIM).astype(jnp.float32)
    scores = jnp.einsum('bqhe,bkhe->bhqk', split_heads[:, :, 0], split_heads[:, :, 1], precision=lax.Precision.HIGHEST) * HEAD_DIM ** (-0.5)
    scores = jnp.where(valid[:, None, None, :], scores, MASKED)
    row_max = lax.optimization_barrier(jnp.max(scores, axis=-1, keepdims=True))
    weights = jnp.exp(scores - row_max)
    weights = (weights / lax.optimization_barrier(jnp.sum(weights, axis=-1, keepdims=True))).astype(jnp.bfloat16)
    context = jnp.einsum('bhqk,bkhe->bqhe', weights.astype(jnp.float32), split_heads[:, :, 2], precision=lax.Precision.HIGHEST)
    context = context.astype(jnp.bfloat16).reshape(block_count * width_len, model_dim)
    mixed = flat_rows.astype(jnp.float32) + jnp.dot(context, w_out, preferred_element_type=jnp.float32)
    return mixed.astype(jnp.bfloat16).reshape(block_count, width_len, model_dim)

def feed_forward(row_data, w_up, w_down):
    shape_in = row_data.shape
    flat_rows = row_data.reshape(-1, shape_in[-1])
    hidden = jax.nn.gelu(jnp.dot(normalize(flat_rows), w_up, preferred_element_type=jnp.float32), approximate=True).astype(jnp.bfloat16)
    result = flat_rows.astype(jnp.float32) + jnp.dot(hidden, w_down, preferred_element_type=jnp.float32)
    return result.astype(jnp.bfloat16).reshape(shape_in)

def reference(points, rank, counts, w_qkv_one, w_out_one, w_up, w_down, w_qkv_two, w_out_two):
    owner_count, group_count, local_points, model_dim = points.shape
    slots_all = OWNER_WINDOWS * WINDOW_SLOTS
    dilation_stride = WINDOW_SLOTS // group_count
    column = jnp.arange(WINDOW_SLOTS, dtype=jnp.int32)
    window_ends = jnp.cumsum(counts, axis=2).astype(jnp.int32)
    starts = (window_ends - counts).astype(jnp.int32)
    usable_mask = column[None, None, None, :] < counts[..., None]
    position = (starts[..., None] + column[None, None, None, :]).astype(jnp.int32)
    owner_base = (jnp.arange(owner_count, dtype=jnp.int32) * local_points)[None, :, None, None]
    sentinel = owner_count * local_points
    sorted_rank = jnp.where(usable_mask, owner_base + position, sentinel).astype(jnp.int32).reshape(group_count, owner_count * slots_all)
    seg_points = jnp.transpose(points, (1, 0, 2, 3)).reshape(group_count, owner_count * local_points, model_dim)
    seg_rank = jnp.transpose(rank, (1, 0, 2)).reshape(group_count, owner_count * local_points).astype(jnp.int32)

    def arrange(row_data, ranks_in, targets):
        ordered = jnp.zeros((sentinel + 1, model_dim), jnp.bfloat16).at[ranks_in].set(row_data)
        return ordered[targets]
    padded = jax.vmap(arrange)(seg_points, seg_rank, sorted_rank)

    def first_block(item_pair):
        row_data, valid = item_pair
        return feed_forward(block_attention(row_data, valid, w_qkv_one, w_out_one), w_up, w_down)
    first_out = lax.map(first_block, (padded.reshape(group_count * owner_count, OWNER_WINDOWS, WINDOW_SLOTS, model_dim), usable_mask.reshape(group_count * owner_count, OWNER_WINDOWS, WINDOW_SLOTS)))
    first_out = first_out.reshape(group_count, owner_count, OWNER_WINDOWS, dilation_stride, group_count, model_dim)
    dilated_input = jnp.transpose(first_out, (1, 4, 2, 0, 3, 5)).reshape(owner_count * group_count, OWNER_WINDOWS, WINDOW_SLOTS, model_dim)
    dilated_valid_mask = jnp.transpose(usable_mask.reshape(group_count, owner_count, OWNER_WINDOWS, dilation_stride, group_count), (1, 4, 2, 0, 3)).reshape(owner_count * group_count, OWNER_WINDOWS, WINDOW_SLOTS)

    def dilated_window_block(item_pair):
        row_data, valid = item_pair
        return block_attention(row_data, valid, w_qkv_two, w_out_two)
    second_result = lax.map(dilated_window_block, (dilated_input, dilated_valid_mask))
    second_result = second_result.reshape(owner_count, group_count, OWNER_WINDOWS, group_count, dilation_stride, model_dim)
    restored = jnp.transpose(second_result, (3, 0, 2, 4, 1, 5)).reshape(group_count, owner_count * slots_all, model_dim)

    def collect(row_data, targets, ranks_in):
        ordered = jnp.zeros((sentinel + 1, model_dim), jnp.bfloat16).at[targets].set(row_data)
        return ordered[ranks_in]
    encoded = jax.vmap(collect)(restored, sorted_rank, seg_rank)
    return jnp.transpose(encoded.reshape(group_count, owner_count, local_points, model_dim), (1, 0, 2, 3))
```

```python
import jax
import jax.numpy as jnp
from jax import lax
from jax.sharding import PartitionSpec as P

HEAD_DIM = 32
WINDOW_SLOTS = 128


EPSILON = 1e-05
MASKED = -1e30


def normalize(row_data):
    values = row_data.astype(jnp.float32)
    center = values - jnp.mean(values, axis=-1, keepdims=True)
    spread = jnp.mean(center * center, axis=-1, keepdims=True)
    return (center * lax.rsqrt(spread + EPSILON)).astype(jnp.bfloat16)


def project(row_data, weight):
    return jnp.dot(normalize(row_data), weight, preferred_element_type=jnp.float32).astype(
        jnp.bfloat16
    )


def attention_core(packed, valid):
    block_count, width_len, triple = packed.shape
    model_dim = triple // 3
    heads_count = model_dim // HEAD_DIM
    split_heads = packed.reshape(block_count, width_len, 3, heads_count, HEAD_DIM)
    scores = jnp.einsum(
        "bqhe,bkhe->bhqk",
        split_heads[:, :, 0],
        split_heads[:, :, 1],
        preferred_element_type=jnp.float32,
    ) * HEAD_DIM ** (-0.5)
    scores = jnp.where(valid[:, None, None, :], scores, MASKED)
    row_max = jnp.max(scores, axis=-1, keepdims=True)
    weights = jnp.exp(scores - row_max)
    weights = (weights / jnp.sum(weights, axis=-1, keepdims=True)).astype(jnp.bfloat16)
    context = jnp.einsum(
        "bhqk,bkhe->bqhe", weights, split_heads[:, :, 2], preferred_element_type=jnp.float32
    )
    return context.astype(jnp.bfloat16).reshape(block_count * width_len, model_dim)


def residual_add(row_data, context, weight):
    return (
        row_data.astype(jnp.float32) + jnp.dot(context, weight, preferred_element_type=jnp.float32)
    ).astype(jnp.bfloat16)


def feed_forward(row_data, w_up, w_down):
    hidden = jax.nn.gelu(
        jnp.dot(normalize(row_data), w_up, preferred_element_type=jnp.float32), approximate=True
    ).astype(jnp.bfloat16)
    return (
        row_data.astype(jnp.float32) + jnp.dot(hidden, w_down, preferred_element_type=jnp.float32)
    ).astype(jnp.bfloat16)


def place(onehot, rows):
    return jnp.dot(onehot, rows, preferred_element_type=jnp.float32).astype(jnp.bfloat16)


def place_back(onehot, rows):
    return lax.dot_general(
        onehot, rows, (((0,), (0,)), ((), ())), preferred_element_type=jnp.float32
    ).astype(jnp.bfloat16)


def on_device(points, rank, counts, w_qkv_one, w_out_one, w_up, w_down, w_qkv_two, w_out_two):
    owner_count = lax.axis_size("win")
    group_count = lax.axis_size("grp")
    win_index = lax.axis_index("win")
    grp_index = lax.axis_index("grp")
    local_points = points.shape[2]
    model_dim = points.shape[3]
    blocks = counts.shape[2]
    slots_all = blocks * WINDOW_SLOTS
    capacity = 2 * local_points // owner_count
    buffer_rows = owner_count * capacity
    dilation_stride = WINDOW_SLOTS // group_count
    rows_x = points.reshape(local_points, model_dim)
    point_rank = rank.reshape(local_points)
    all_rank = lax.all_gather(point_rank, "win", axis=0, tiled=False)
    column_counts = lax.dynamic_index_in_dim(counts, grp_index, 0, keepdims=False)

    owner_dev = point_rank // local_points
    owner_ids = jnp.arange(owner_count, dtype=jnp.int32)
    choose = (owner_dev[:, None] == owner_ids[None, :]).astype(jnp.int32)
    peer_order = jnp.sum(choose * (jnp.cumsum(choose, axis=0) - 1), axis=1)
    send_place = owner_dev * capacity + peer_order
    buffer_ids = jnp.arange(buffer_rows, dtype=jnp.int32)
    send_hot = (buffer_ids[:, None] == send_place[None, :]).astype(jnp.bfloat16)
    outgoing = place(send_hot, rows_x)
    arrived = lax.all_to_all(outgoing, "win", split_axis=0, concat_axis=0, tiled=True)

    own_counts = lax.dynamic_index_in_dim(column_counts, win_index, 0, keepdims=False)
    own_ends = jnp.cumsum(own_counts)
    own_starts = own_ends - own_counts
    mine = (all_rank // local_points) == win_index
    mine_i = mine.astype(jnp.int32)
    order = jnp.cumsum(mine_i, axis=1) - 1
    offset = all_rank % local_points
    window = jnp.sum((own_ends[None, None, :] <= offset[:, :, None]).astype(jnp.int32), axis=2)
    block_ids = jnp.arange(blocks, dtype=jnp.int32)
    start_of = jnp.sum(
        (window[:, :, None] == block_ids[None, None, :]).astype(jnp.int32) * own_starts[None, None, :],
        axis=2,
    )
    slot = window * WINDOW_SLOTS + offset - start_of
    cap_ids = jnp.arange(capacity, dtype=jnp.int32)
    pick = (order[:, :, None] == cap_ids[None, None, :]) & mine[:, :, None]
    arrived_slot = jnp.sum(pick.astype(jnp.int32) * (slot[:, :, None] + 1), axis=1) - 1
    slot_ids = jnp.arange(slots_all, dtype=jnp.int32)
    recv_hot = (slot_ids[:, None] == arrived_slot.reshape(1, buffer_rows)).astype(jnp.bfloat16)
    padded_x = place(recv_hot, arrived)

    column = jnp.arange(WINDOW_SLOTS, dtype=jnp.int32)
    usable_mask = column[None, :] < own_counts[:, None]
    packed = project(padded_x, w_qkv_one).reshape(blocks, WINDOW_SLOTS, 3 * model_dim)
    context = attention_core(packed, usable_mask)
    first_pad = feed_forward(residual_add(padded_x, context, w_out_one), w_up, w_down)
    dilated_rows = lax.all_to_all(
        first_pad.reshape(blocks, dilation_stride, group_count, model_dim),
        "grp",
        split_axis=2,
        concat_axis=1,
        tiled=True,
    )
    owner_counts = lax.dynamic_index_in_dim(counts, win_index, 1, keepdims=False)
    k_ids = jnp.arange(dilation_stride, dtype=jnp.int32)
    valid_marks = (k_ids[None, None, :] * group_count + grp_index) < jnp.transpose(owner_counts)[
        :, :, None
    ]
    block_count = dilated_rows.shape[0]
    flat_rows = dilated_rows.reshape(block_count * WINDOW_SLOTS, model_dim)
    packed_two = project(flat_rows, w_qkv_two).reshape(block_count, WINDOW_SLOTS, 3 * model_dim)
    head_context = attention_core(packed_two, valid_marks.reshape(block_count, WINDOW_SLOTS))
    mixed_rows = residual_add(flat_rows, head_context, w_out_two).reshape(
        block_count, WINDOW_SLOTS, 1, model_dim
    )
    second_pad = lax.all_to_all(mixed_rows, "grp", split_axis=1, concat_axis=2, tiled=True).reshape(
        slots_all, model_dim
    )
    returning = place_back(recv_hot, second_pad)
    returned = lax.all_to_all(returning, "win", split_axis=0, concat_axis=0, tiled=True)
    encoded = place_back(send_hot, returned)
    return encoded.reshape(1, 1, local_points, model_dim)


def solution(mesh):
    return jax.shard_map(
        on_device,
        mesh=mesh,
        in_specs=(
            P("win", "grp", None, None),
            P("win", "grp", None),
            P(),
            P(),
            P(),
            P(),
            P(),
            P(),
            P(),
        ),
        out_specs=P("win", "grp", None, None),
        check_vma=False,
    )
```

```python
import jax
import jax.numpy as jnp
from jax import lax
from jax.sharding import PartitionSpec as P

HEAD_DIM = 32
WINDOW_SLOTS = 128


EPSILON = 1e-05
MASKED = -1e30


def normalize(row_data):
    values = row_data.astype(jnp.float32)
    center = values - jnp.mean(values, axis=-1, keepdims=True)
    spread = jnp.mean(center * center, axis=-1, keepdims=True)
    return (center * lax.rsqrt(spread + EPSILON)).astype(jnp.bfloat16)


def project(row_data, weight):
    return jnp.dot(normalize(row_data), weight, preferred_element_type=jnp.float32).astype(
        jnp.bfloat16
    )


def attention_core(packed, valid):
    block_count, width_len, triple = packed.shape
    model_dim = triple // 3
    heads_count = model_dim // HEAD_DIM
    split_heads = packed.reshape(block_count, width_len, 3, heads_count, HEAD_DIM)
    scores = jnp.einsum(
        "bqhe,bkhe->bhqk",
        split_heads[:, :, 0],
        split_heads[:, :, 1],
        preferred_element_type=jnp.float32,
    ) * HEAD_DIM ** (-0.5)
    scores = jnp.where(valid[:, None, None, :], scores, MASKED)
    row_max = jnp.max(scores, axis=-1, keepdims=True)
    weights = jnp.exp(scores - row_max)
    weights = (weights / jnp.sum(weights, axis=-1, keepdims=True)).astype(jnp.bfloat16)
    context = jnp.einsum(
        "bhqk,bkhe->bqhe", weights, split_heads[:, :, 2], preferred_element_type=jnp.float32
    )
    return context.astype(jnp.bfloat16).reshape(block_count * width_len, model_dim)


def residual_add(row_data, context, weight):
    return (
        row_data.astype(jnp.float32) + jnp.dot(context, weight, preferred_element_type=jnp.float32)
    ).astype(jnp.bfloat16)


def feed_forward(row_data, w_up, w_down):
    hidden = jax.nn.gelu(
        jnp.dot(normalize(row_data), w_up, preferred_element_type=jnp.float32), approximate=True
    ).astype(jnp.bfloat16)
    return (
        row_data.astype(jnp.float32) + jnp.dot(hidden, w_down, preferred_element_type=jnp.float32)
    ).astype(jnp.bfloat16)


def place(onehot, rows):
    return jnp.dot(onehot, rows, preferred_element_type=jnp.float32).astype(jnp.bfloat16)


def place_back(onehot, rows):
    return lax.dot_general(
        onehot, rows, (((0,), (0,)), ((), ())), preferred_element_type=jnp.float32
    ).astype(jnp.bfloat16)


def on_device(points, rank, counts, w_qkv_one, w_out_one, w_up, w_down, w_qkv_two, w_out_two):
    owner_count = lax.axis_size("win")
    group_count = lax.axis_size("grp")
    win_index = lax.axis_index("win")
    grp_index = lax.axis_index("grp")
    local_points = points.shape[2]
    model_dim = points.shape[3]
    blocks = counts.shape[2]
    slots_all = blocks * WINDOW_SLOTS
    capacity = 2 * local_points // owner_count
    buffer_rows = owner_count * capacity
    dilation_stride = WINDOW_SLOTS // group_count
    rows_x = points.reshape(local_points, model_dim)
    point_rank = rank.reshape(local_points)
    column_counts = lax.dynamic_index_in_dim(counts, grp_index, 0, keepdims=False)

    owner_dev = point_rank // local_points
    owner_ids = jnp.arange(owner_count, dtype=jnp.int32)
    choose = (owner_dev[:, None] == owner_ids[None, :]).astype(jnp.int32)
    peer_order = jnp.sum(choose * (jnp.cumsum(choose, axis=0) - 1), axis=1)
    send_place = owner_dev * capacity + peer_order
    buffer_ids = jnp.arange(buffer_rows, dtype=jnp.int32)
    send_hot = (buffer_ids[:, None] == send_place[None, :]).astype(jnp.bfloat16)
    outgoing = place(send_hot, rows_x)
    arrived = lax.all_to_all(outgoing, "win", split_axis=0, concat_axis=0, tiled=True)

    window_ends = jnp.cumsum(column_counts, axis=1)
    starts = window_ends - column_counts
    offset = point_rank % local_points
    owner_ends = jnp.sum(choose[:, :, None] * window_ends[None], axis=1)
    owner_starts = jnp.sum(choose[:, :, None] * starts[None], axis=1)
    window = jnp.sum((owner_ends <= offset[:, None]).astype(jnp.int32), axis=1)
    block_ids = jnp.arange(blocks, dtype=jnp.int32)
    block_pick = (window[:, None] == block_ids[None, :]).astype(jnp.int32)
    dest_slot = window * WINDOW_SLOTS + offset - jnp.sum(block_pick * owner_starts, axis=1)
    outgoing_slot = jnp.sum(send_hot.astype(jnp.int32) * (dest_slot[None, :] + 1), axis=1) - 1
    arrived_slot = lax.all_to_all(
        outgoing_slot.reshape(owner_count, capacity), "win", split_axis=0, concat_axis=0, tiled=True
    )
    own_counts = lax.dynamic_index_in_dim(column_counts, win_index, 0, keepdims=False)
    slot_ids = jnp.arange(slots_all, dtype=jnp.int32)
    recv_hot = (slot_ids[:, None] == arrived_slot.reshape(1, buffer_rows)).astype(jnp.bfloat16)
    padded_x = place(recv_hot, arrived)

    column = jnp.arange(WINDOW_SLOTS, dtype=jnp.int32)
    usable_mask = column[None, :] < own_counts[:, None]
    packed = project(padded_x, w_qkv_one).reshape(blocks, WINDOW_SLOTS, 3 * model_dim)
    context = attention_core(packed, usable_mask)
    first_pad = feed_forward(residual_add(padded_x, context, w_out_one), w_up, w_down)
    dilated_rows = lax.all_to_all(
        first_pad.reshape(blocks, dilation_stride, group_count, model_dim),
        "grp",
        split_axis=2,
        concat_axis=1,
        tiled=True,
    )
    owner_counts = lax.dynamic_index_in_dim(counts, win_index, 1, keepdims=False)
    k_ids = jnp.arange(dilation_stride, dtype=jnp.int32)
    valid_marks = (k_ids[None, None, :] * group_count + grp_index) < jnp.transpose(owner_counts)[
        :, :, None
    ]
    block_count = dilated_rows.shape[0]
    flat_rows = dilated_rows.reshape(block_count * WINDOW_SLOTS, model_dim)
    packed_two = project(flat_rows, w_qkv_two).reshape(block_count, WINDOW_SLOTS, 3 * model_dim)
    head_context = attention_core(packed_two, valid_marks.reshape(block_count, WINDOW_SLOTS))
    mixed_rows = residual_add(flat_rows, head_context, w_out_two).reshape(
        block_count, WINDOW_SLOTS, 1, model_dim
    )
    second_pad = lax.all_to_all(mixed_rows, "grp", split_axis=1, concat_axis=2, tiled=True).reshape(
        slots_all, model_dim
    )
    returning = place_back(recv_hot, second_pad)
    returned = lax.all_to_all(returning, "win", split_axis=0, concat_axis=0, tiled=True)
    encoded = place_back(send_hot, returned)
    return encoded.reshape(1, 1, local_points, model_dim)


def solution(mesh):
    return jax.shard_map(
        on_device,
        mesh=mesh,
        in_specs=(
            P("win", "grp", None, None),
            P("win", "grp", None),
            P(),
            P(),
            P(),
            P(),
            P(),
            P(),
            P(),
        ),
        out_specs=P("win", "grp", None, None),
        check_vma=False,
    )
```

```python
import jax
import jax.numpy as jnp
from jax import lax
from jax.sharding import PartitionSpec as P

HEAD_DIM = 32
WINDOW_SLOTS = 128


EPSILON = 1e-05
MASKED = -1e30
CHUNKS = 2


def normalize(row_data):
    values = row_data.astype(jnp.float32)
    center = values - jnp.mean(values, axis=-1, keepdims=True)
    spread = jnp.mean(center * center, axis=-1, keepdims=True)
    return (center * lax.rsqrt(spread + EPSILON)).astype(jnp.bfloat16)


def project(row_data, weight):
    return jnp.dot(normalize(row_data), weight, preferred_element_type=jnp.float32).astype(
        jnp.bfloat16
    )


def attention_core(packed, valid):
    block_count, width_len, triple = packed.shape
    model_dim = triple // 3
    heads_count = model_dim // HEAD_DIM
    split_heads = packed.reshape(block_count, width_len, 3, heads_count, HEAD_DIM)
    scores = jnp.einsum(
        "bqhe,bkhe->bhqk",
        split_heads[:, :, 0],
        split_heads[:, :, 1],
        preferred_element_type=jnp.float32,
    ) * HEAD_DIM ** (-0.5)
    scores = jnp.where(valid[:, None, None, :], scores, MASKED)
    row_max = jnp.max(scores, axis=-1, keepdims=True)
    weights = jnp.exp(scores - row_max)
    weights = (weights / jnp.sum(weights, axis=-1, keepdims=True)).astype(jnp.bfloat16)
    context = jnp.einsum(
        "bhqk,bkhe->bqhe", weights, split_heads[:, :, 2], preferred_element_type=jnp.float32
    )
    return context.astype(jnp.bfloat16).reshape(block_count * width_len, model_dim)


def residual_add(row_data, context, weight):
    return (
        row_data.astype(jnp.float32) + jnp.dot(context, weight, preferred_element_type=jnp.float32)
    ).astype(jnp.bfloat16)


def feed_forward(row_data, w_up, w_down):
    hidden = jax.nn.gelu(
        jnp.dot(normalize(row_data), w_up, preferred_element_type=jnp.float32), approximate=True
    ).astype(jnp.bfloat16)
    return (
        row_data.astype(jnp.float32) + jnp.dot(hidden, w_down, preferred_element_type=jnp.float32)
    ).astype(jnp.bfloat16)


def place(onehot, rows):
    return jnp.dot(onehot, rows, preferred_element_type=jnp.float32).astype(jnp.bfloat16)


def place_back(onehot, rows):
    return lax.dot_general(
        onehot, rows, (((0,), (0,)), ((), ())), preferred_element_type=jnp.float32
    ).astype(jnp.bfloat16)


def on_device(points, rank, counts, w_qkv_one, w_out_one, w_up, w_down, w_qkv_two, w_out_two):
    owner_count = lax.axis_size("win")
    group_count = lax.axis_size("grp")
    win_index = lax.axis_index("win")
    grp_index = lax.axis_index("grp")
    local_points = points.shape[2]
    model_dim = points.shape[3]
    blocks = counts.shape[2]
    slots_all = blocks * WINDOW_SLOTS
    capacity = 2 * local_points // owner_count
    buffer_rows = owner_count * capacity
    dilation_stride = WINDOW_SLOTS // group_count
    rows_x = points.reshape(local_points, model_dim)
    point_rank = rank.reshape(local_points)
    column_counts = lax.dynamic_index_in_dim(counts, grp_index, 0, keepdims=False)

    owner_dev = point_rank // local_points
    owner_ids = jnp.arange(owner_count, dtype=jnp.int32)
    choose = (owner_dev[:, None] == owner_ids[None, :]).astype(jnp.int32)
    peer_order = jnp.sum(choose * (jnp.cumsum(choose, axis=0) - 1), axis=1)
    send_place = owner_dev * capacity + peer_order
    buffer_ids = jnp.arange(buffer_rows, dtype=jnp.int32)
    send_hot = (buffer_ids[:, None] == send_place[None, :]).astype(jnp.bfloat16)
    outgoing = place(send_hot, rows_x)
    arrived = lax.all_to_all(outgoing, "win", split_axis=0, concat_axis=0, tiled=True)

    window_ends = jnp.cumsum(column_counts, axis=1)
    starts = window_ends - column_counts
    offset = point_rank % local_points
    owner_ends = jnp.sum(choose[:, :, None] * window_ends[None], axis=1)
    owner_starts = jnp.sum(choose[:, :, None] * starts[None], axis=1)
    window = jnp.sum((owner_ends <= offset[:, None]).astype(jnp.int32), axis=1)
    block_ids = jnp.arange(blocks, dtype=jnp.int32)
    block_pick = (window[:, None] == block_ids[None, :]).astype(jnp.int32)
    dest_slot = window * WINDOW_SLOTS + offset - jnp.sum(block_pick * owner_starts, axis=1)
    outgoing_slot = jnp.sum(send_hot.astype(jnp.int32) * (dest_slot[None, :] + 1), axis=1) - 1
    arrived_slot = lax.all_to_all(
        outgoing_slot.reshape(owner_count, capacity), "win", split_axis=0, concat_axis=0, tiled=True
    )
    own_counts = lax.dynamic_index_in_dim(column_counts, win_index, 0, keepdims=False)
    slot_ids = jnp.arange(slots_all, dtype=jnp.int32)
    recv_hot = (slot_ids[:, None] == arrived_slot.reshape(1, buffer_rows)).astype(jnp.bfloat16)
    padded_x = place(recv_hot, arrived)

    column = jnp.arange(WINDOW_SLOTS, dtype=jnp.int32)
    usable_mask = column[None, :] < own_counts[:, None]
    owner_counts = lax.dynamic_index_in_dim(counts, win_index, 1, keepdims=False)
    k_ids = jnp.arange(dilation_stride, dtype=jnp.int32)
    valid_marks = (k_ids[None, None, :] * group_count + grp_index) < jnp.transpose(owner_counts)[
        :, :, None
    ]
    valid_marks = valid_marks.reshape(blocks, WINDOW_SLOTS)
    padded_blocks = padded_x.reshape(blocks, WINDOW_SLOTS, model_dim)
    per = blocks // CHUNKS
    pieces = []
    for chunk in range(CHUNKS):
        low, high = chunk * per, (chunk + 1) * per
        chunk_x = padded_blocks[low:high].reshape(per * WINDOW_SLOTS, model_dim)
        packed = project(chunk_x, w_qkv_one).reshape(per, WINDOW_SLOTS, 3 * model_dim)
        context = attention_core(packed, usable_mask[low:high])
        first_pad = feed_forward(residual_add(chunk_x, context, w_out_one), w_up, w_down)
        dilated_rows = lax.all_to_all(
            first_pad.reshape(per, dilation_stride, group_count, model_dim),
            "grp",
            split_axis=2,
            concat_axis=1,
            tiled=True,
        )
        flat_rows = dilated_rows.reshape(per * WINDOW_SLOTS, model_dim)
        packed_two = project(flat_rows, w_qkv_two).reshape(per, WINDOW_SLOTS, 3 * model_dim)
        head_context = attention_core(packed_two, valid_marks[low:high])
        mixed_rows = residual_add(flat_rows, head_context, w_out_two).reshape(
            per, WINDOW_SLOTS, 1, model_dim
        )
        pieces.append(lax.all_to_all(mixed_rows, "grp", split_axis=1, concat_axis=2, tiled=True))
    second_pad = jnp.concatenate(pieces, axis=0).reshape(slots_all, model_dim)
    returning = place_back(recv_hot, second_pad)
    returned = lax.all_to_all(returning, "win", split_axis=0, concat_axis=0, tiled=True)
    encoded = place_back(send_hot, returned)
    return encoded.reshape(1, 1, local_points, model_dim)


def solution(mesh):
    return jax.shard_map(
        on_device,
        mesh=mesh,
        in_specs=(
            P("win", "grp", None, None),
            P("win", "grp", None),
            P(),
            P(),
            P(),
            P(),
            P(),
            P(),
            P(),
        ),
        out_specs=P("win", "grp", None, None),
        check_vma=False,
    )
```

```python
import jax
import jax.numpy as jnp
from jax import lax
from jax.sharding import PartitionSpec as P

HEAD_DIM = 32
WINDOW_SLOTS = 128


EPSILON = 1e-05
MASKED = -1e30


def normalize(row_data):
    values = row_data.astype(jnp.float32)
    center = values - jnp.mean(values, axis=-1, keepdims=True)
    spread = jnp.mean(center * center, axis=-1, keepdims=True)
    return (center * lax.rsqrt(spread + EPSILON)).astype(jnp.bfloat16)


def project(row_data, weight):
    return jnp.dot(normalize(row_data), weight, preferred_element_type=jnp.float32).astype(
        jnp.bfloat16
    )


def attention_block(row_data, valid, w_qkv, w_out):
    rows_count, model_dim = row_data.shape
    heads_count = model_dim // HEAD_DIM
    block_count = rows_count // WINDOW_SLOTS
    normed = normalize(row_data)
    w_split = w_qkv.reshape(model_dim, 3, heads_count, HEAD_DIM)

    def head_major(part):
        out = jnp.einsum("nd,dhe->hne", normed, w_split[:, part], preferred_element_type=jnp.float32)
        return out.astype(jnp.bfloat16).reshape(heads_count, block_count, WINDOW_SLOTS, HEAD_DIM)

    query, key, value = head_major(0), head_major(1), head_major(2)
    scores = jnp.einsum(
        "hbqe,hbke->hbqk", query, key, preferred_element_type=jnp.float32
    ) * HEAD_DIM ** (-0.5)
    scores = jnp.where(valid[None, :, None, :], scores, MASKED)
    row_max = jnp.max(scores, axis=-1, keepdims=True)
    weights = jnp.exp(scores - row_max)
    weights = (weights / jnp.sum(weights, axis=-1, keepdims=True)).astype(jnp.bfloat16)
    context = jnp.einsum("hbqk,hbke->hbqe", weights, value, preferred_element_type=jnp.float32)
    context = context.astype(jnp.bfloat16).reshape(heads_count, rows_count, HEAD_DIM)
    mixed = jnp.einsum(
        "hne,hed->nd",
        context,
        w_out.reshape(heads_count, HEAD_DIM, model_dim),
        preferred_element_type=jnp.float32,
    )
    return (row_data.astype(jnp.float32) + mixed).astype(jnp.bfloat16)


def feed_forward(row_data, w_up, w_down):
    hidden = jax.nn.gelu(
        jnp.dot(normalize(row_data), w_up, preferred_element_type=jnp.float32), approximate=True
    ).astype(jnp.bfloat16)
    return (
        row_data.astype(jnp.float32) + jnp.dot(hidden, w_down, preferred_element_type=jnp.float32)
    ).astype(jnp.bfloat16)


def place(onehot, rows):
    return jnp.dot(onehot, rows, preferred_element_type=jnp.float32).astype(jnp.bfloat16)


def place_back(onehot, rows):
    return lax.dot_general(
        onehot, rows, (((0,), (0,)), ((), ())), preferred_element_type=jnp.float32
    ).astype(jnp.bfloat16)


def on_device(points, rank, counts, w_qkv_one, w_out_one, w_up, w_down, w_qkv_two, w_out_two):
    owner_count = lax.axis_size("win")
    group_count = lax.axis_size("grp")
    win_index = lax.axis_index("win")
    grp_index = lax.axis_index("grp")
    local_points = points.shape[2]
    model_dim = points.shape[3]
    blocks = counts.shape[2]
    slots_all = blocks * WINDOW_SLOTS
    capacity = 2 * local_points // owner_count
    buffer_rows = owner_count * capacity
    dilation_stride = WINDOW_SLOTS // group_count
    rows_x = points.reshape(local_points, model_dim)
    point_rank = rank.reshape(local_points)
    column_counts = lax.dynamic_index_in_dim(counts, grp_index, 0, keepdims=False)

    owner_dev = point_rank // local_points
    owner_ids = jnp.arange(owner_count, dtype=jnp.int32)
    choose = (owner_dev[:, None] == owner_ids[None, :]).astype(jnp.int32)
    peer_order = jnp.sum(choose * (jnp.cumsum(choose, axis=0) - 1), axis=1)
    send_place = owner_dev * capacity + peer_order
    buffer_ids = jnp.arange(buffer_rows, dtype=jnp.int32)
    send_hot = (buffer_ids[:, None] == send_place[None, :]).astype(jnp.bfloat16)
    outgoing = place(send_hot, rows_x)
    arrived = lax.all_to_all(outgoing, "win", split_axis=0, concat_axis=0, tiled=True)

    window_ends = jnp.cumsum(column_counts, axis=1)
    starts = window_ends - column_counts
    offset = point_rank % local_points
    owner_ends = jnp.sum(choose[:, :, None] * window_ends[None], axis=1)
    owner_starts = jnp.sum(choose[:, :, None] * starts[None], axis=1)
    window = jnp.sum((owner_ends <= offset[:, None]).astype(jnp.int32), axis=1)
    block_ids = jnp.arange(blocks, dtype=jnp.int32)
    block_pick = (window[:, None] == block_ids[None, :]).astype(jnp.int32)
    dest_slot = window * WINDOW_SLOTS + offset - jnp.sum(block_pick * owner_starts, axis=1)
    outgoing_slot = jnp.sum(send_hot.astype(jnp.int32) * (dest_slot[None, :] + 1), axis=1) - 1
    arrived_slot = lax.all_to_all(
        outgoing_slot.reshape(owner_count, capacity), "win", split_axis=0, concat_axis=0, tiled=True
    )
    own_counts = lax.dynamic_index_in_dim(column_counts, win_index, 0, keepdims=False)
    slot_ids = jnp.arange(slots_all, dtype=jnp.int32)
    recv_hot = (slot_ids[:, None] == arrived_slot.reshape(1, buffer_rows)).astype(jnp.bfloat16)
    padded_x = place(recv_hot, arrived)

    column = jnp.arange(WINDOW_SLOTS, dtype=jnp.int32)
    usable_mask = column[None, :] < own_counts[:, None]
    first_pad = feed_forward(attention_block(padded_x, usable_mask, w_qkv_one, w_out_one), w_up, w_down)
    dilated_rows = lax.all_to_all(
        first_pad.reshape(blocks, dilation_stride, group_count, model_dim),
        "grp",
        split_axis=2,
        concat_axis=1,
        tiled=True,
    )
    owner_counts = lax.dynamic_index_in_dim(counts, win_index, 1, keepdims=False)
    k_ids = jnp.arange(dilation_stride, dtype=jnp.int32)
    valid_marks = (k_ids[None, None, :] * group_count + grp_index) < jnp.transpose(owner_counts)[
        :, :, None
    ]
    block_count = dilated_rows.shape[0]
    flat_rows = dilated_rows.reshape(block_count * WINDOW_SLOTS, model_dim)
    mixed_rows = attention_block(
        flat_rows, valid_marks.reshape(block_count, WINDOW_SLOTS), w_qkv_two, w_out_two
    ).reshape(
        block_count, WINDOW_SLOTS, 1, model_dim
    )
    second_pad = lax.all_to_all(mixed_rows, "grp", split_axis=1, concat_axis=2, tiled=True).reshape(
        slots_all, model_dim
    )
    returning = place_back(recv_hot, second_pad)
    returned = lax.all_to_all(returning, "win", split_axis=0, concat_axis=0, tiled=True)
    encoded = place_back(send_hot, returned)
    return encoded.reshape(1, 1, local_points, model_dim)


def solution(mesh):
    return jax.shard_map(
        on_device,
        mesh=mesh,
        in_specs=(
            P("win", "grp", None, None),
            P("win", "grp", None),
            P(),
            P(),
            P(),
            P(),
            P(),
            P(),
            P(),
        ),
        out_specs=P("win", "grp", None, None),
        check_vma=False,
    )
```

```python
import jax
import jax.numpy as jnp
from jax import lax
from jax.sharding import PartitionSpec as P

HEAD_DIM = 32
WINDOW_SLOTS = 128


EPSILON = 1e-05
MASKED = -1e30
SLOT_BASE = 32
TAIL = 128


def normalize(row_data):
    values = row_data.astype(jnp.float32)
    center = values - jnp.mean(values, axis=-1, keepdims=True)
    spread = jnp.mean(center * center, axis=-1, keepdims=True)
    return (center * lax.rsqrt(spread + EPSILON)).astype(jnp.bfloat16)


def project(row_data, weight):
    return jnp.dot(normalize(row_data), weight, preferred_element_type=jnp.float32).astype(
        jnp.bfloat16
    )


def attention_block(row_data, valid, w_qkv, w_out):
    rows_count, model_dim = row_data.shape
    heads_count = model_dim // HEAD_DIM
    block_count = rows_count // WINDOW_SLOTS
    normed = normalize(row_data)
    w_split = w_qkv.reshape(model_dim, 3, heads_count, HEAD_DIM)

    def head_major(part):
        out = jnp.einsum("nd,dhe->hne", normed, w_split[:, part], preferred_element_type=jnp.float32)
        return out.astype(jnp.bfloat16).reshape(heads_count, block_count, WINDOW_SLOTS, HEAD_DIM)

    query, key, value = head_major(0), head_major(1), head_major(2)
    scores = jnp.einsum(
        "hbqe,hbke->hbqk", query, key, preferred_element_type=jnp.float32
    ) * HEAD_DIM ** (-0.5)
    scores = jnp.where(valid[None, :, None, :], scores, MASKED)
    row_max = jnp.max(scores, axis=-1, keepdims=True)
    weights = jnp.exp(scores - row_max)
    weights = (weights / jnp.sum(weights, axis=-1, keepdims=True)).astype(jnp.bfloat16)
    context = jnp.einsum("hbqk,hbke->hbqe", weights, value, preferred_element_type=jnp.float32)
    context = context.astype(jnp.bfloat16).reshape(heads_count, rows_count, HEAD_DIM)
    mixed = jnp.einsum(
        "hne,hed->nd",
        context,
        w_out.reshape(heads_count, HEAD_DIM, model_dim),
        preferred_element_type=jnp.float32,
    )
    return (row_data.astype(jnp.float32) + mixed).astype(jnp.bfloat16)


def feed_forward(row_data, w_up, w_down):
    hidden = jax.nn.gelu(
        jnp.dot(normalize(row_data), w_up, preferred_element_type=jnp.float32), approximate=True
    ).astype(jnp.bfloat16)
    return (
        row_data.astype(jnp.float32) + jnp.dot(hidden, w_down, preferred_element_type=jnp.float32)
    ).astype(jnp.bfloat16)


def place(onehot, rows):
    return jnp.dot(onehot, rows, preferred_element_type=jnp.float32).astype(jnp.bfloat16)


def place_back(onehot, rows):
    return lax.dot_general(
        onehot, rows, (((0,), (0,)), ((), ())), preferred_element_type=jnp.float32
    ).astype(jnp.bfloat16)


def on_device(points, rank, counts, w_qkv_one, w_out_one, w_up, w_down, w_qkv_two, w_out_two):
    owner_count = lax.axis_size("win")
    group_count = lax.axis_size("grp")
    win_index = lax.axis_index("win")
    grp_index = lax.axis_index("grp")
    local_points = points.shape[2]
    model_dim = points.shape[3]
    blocks = counts.shape[2]
    slots_all = blocks * WINDOW_SLOTS
    capacity = 2 * local_points // owner_count
    buffer_rows = owner_count * capacity
    dilation_stride = WINDOW_SLOTS // group_count
    rows_x = points.reshape(local_points, model_dim)
    point_rank = rank.reshape(local_points)
    column_counts = lax.dynamic_index_in_dim(counts, grp_index, 0, keepdims=False)

    owner_dev = point_rank // local_points
    owner_ids = jnp.arange(owner_count, dtype=jnp.int32)
    choose = (owner_dev[:, None] == owner_ids[None, :]).astype(jnp.int32)
    peer_order = jnp.sum(choose * (jnp.cumsum(choose, axis=0) - 1), axis=1)
    send_place = owner_dev * capacity + peer_order
    buffer_ids = jnp.arange(buffer_rows, dtype=jnp.int32)
    send_hot = (buffer_ids[:, None] == send_place[None, :]).astype(jnp.bfloat16)
    outgoing = place(send_hot, rows_x)

    window_ends = jnp.cumsum(column_counts, axis=1)
    starts = window_ends - column_counts
    offset = point_rank % local_points
    owner_ends = jnp.sum(choose[:, :, None] * window_ends[None], axis=1)
    owner_starts = jnp.sum(choose[:, :, None] * starts[None], axis=1)
    window = jnp.sum((owner_ends <= offset[:, None]).astype(jnp.int32), axis=1)
    block_ids = jnp.arange(blocks, dtype=jnp.int32)
    block_pick = (window[:, None] == block_ids[None, :]).astype(jnp.int32)
    dest_slot = window * WINDOW_SLOTS + offset - jnp.sum(block_pick * owner_starts, axis=1)
    slot_code = jnp.sum(send_hot.astype(jnp.int32) * (dest_slot[None, :] + 1), axis=1)
    slot_code = slot_code.reshape(owner_count, capacity)
    code_tail = jnp.concatenate(
        [slot_code // SLOT_BASE, slot_code % SLOT_BASE], axis=1
    ).astype(jnp.bfloat16)
    code_tail = jnp.pad(code_tail, ((0, 0), (0, TAIL - 2 * capacity)))
    sending = jnp.concatenate(
        [outgoing.reshape(owner_count, capacity * model_dim), code_tail], axis=1
    )
    receiving = lax.all_to_all(sending, "win", split_axis=0, concat_axis=0, tiled=True)
    arrived = receiving[:, : capacity * model_dim].reshape(buffer_rows, model_dim)
    code_back = receiving[:, capacity * model_dim :].astype(jnp.int32)
    arrived_slot = code_back[:, :capacity] * SLOT_BASE + code_back[:, capacity : 2 * capacity] - 1
    own_counts = lax.dynamic_index_in_dim(column_counts, win_index, 0, keepdims=False)
    slot_ids = jnp.arange(slots_all, dtype=jnp.int32)
    recv_hot = (slot_ids[:, None] == arrived_slot.reshape(1, buffer_rows)).astype(jnp.bfloat16)
    padded_x = place(recv_hot, arrived)

    column = jnp.arange(WINDOW_SLOTS, dtype=jnp.int32)
    usable_mask = column[None, :] < own_counts[:, None]
    first_pad = feed_forward(attention_block(padded_x, usable_mask, w_qkv_one, w_out_one), w_up, w_down)
    dilated_rows = lax.all_to_all(
        first_pad.reshape(blocks, dilation_stride, group_count, model_dim),
        "grp",
        split_axis=2,
        concat_axis=1,
        tiled=True,
    )
    owner_counts = lax.dynamic_index_in_dim(counts, win_index, 1, keepdims=False)
    k_ids = jnp.arange(dilation_stride, dtype=jnp.int32)
    valid_marks = (k_ids[None, None, :] * group_count + grp_index) < jnp.transpose(owner_counts)[
        :, :, None
    ]
    block_count = dilated_rows.shape[0]
    flat_rows = dilated_rows.reshape(block_count * WINDOW_SLOTS, model_dim)
    mixed_rows = attention_block(
        flat_rows, valid_marks.reshape(block_count, WINDOW_SLOTS), w_qkv_two, w_out_two
    ).reshape(
        block_count, WINDOW_SLOTS, 1, model_dim
    )
    second_pad = lax.all_to_all(mixed_rows, "grp", split_axis=1, concat_axis=2, tiled=True).reshape(
        slots_all, model_dim
    )
    returning = place_back(recv_hot, second_pad)
    returned = lax.all_to_all(returning, "win", split_axis=0, concat_axis=0, tiled=True)
    encoded = place_back(send_hot, returned)
    return encoded.reshape(1, 1, local_points, model_dim)


def solution(mesh):
    return jax.shard_map(
        on_device,
        mesh=mesh,
        in_specs=(
            P("win", "grp", None, None),
            P("win", "grp", None),
            P(),
            P(),
            P(),
            P(),
            P(),
            P(),
            P(),
        ),
        out_specs=P("win", "grp", None, None),
        check_vma=False,
    )
```

```python
import jax
import jax.numpy as jnp
from jax import lax
from jax.sharding import PartitionSpec as P

HEAD_DIM = 32
WINDOW_SLOTS = 128


EPSILON = 1e-05
MASKED = -1e30
SLOT_BASE = 32
TAIL = 128


def normalize(row_data):
    values = row_data.astype(jnp.float32)
    center = values - jnp.mean(values, axis=-1, keepdims=True)
    spread = jnp.mean(center * center, axis=-1, keepdims=True)
    return (center * lax.rsqrt(spread + EPSILON)).astype(jnp.bfloat16)


def project(row_data, weight):
    return jnp.dot(normalize(row_data), weight, preferred_element_type=jnp.float32).astype(
        jnp.bfloat16
    )


def attention_block(row_data, valid, w_qkv, w_out):
    rows_count, model_dim = row_data.shape
    heads_count = model_dim // HEAD_DIM
    block_count = rows_count // WINDOW_SLOTS
    normed = normalize(row_data)
    w_split = w_qkv.reshape(model_dim, 3, heads_count, HEAD_DIM)

    def head_major(part):
        out = jnp.einsum("nd,dhe->hne", normed, w_split[:, part], preferred_element_type=jnp.float32)
        return out.astype(jnp.bfloat16).reshape(heads_count, block_count, WINDOW_SLOTS, HEAD_DIM)

    query, key, value = head_major(0), head_major(1), head_major(2)
    scores = jnp.einsum(
        "hbqe,hbke->hbqk", query, key, preferred_element_type=jnp.float32
    ) * HEAD_DIM ** (-0.5)
    scores = jnp.where(valid[None, :, None, :], scores, MASKED)
    row_max = jnp.max(scores, axis=-1, keepdims=True)
    weights = jnp.exp(scores - row_max)
    weights = (weights / jnp.sum(weights, axis=-1, keepdims=True)).astype(jnp.bfloat16)
    context = jnp.einsum("hbqk,hbke->hbqe", weights, value, preferred_element_type=jnp.float32)
    context = context.astype(jnp.bfloat16).reshape(heads_count, rows_count, HEAD_DIM)
    mixed = jnp.einsum(
        "hne,hed->nd",
        context,
        w_out.reshape(heads_count, HEAD_DIM, model_dim),
        preferred_element_type=jnp.float32,
    )
    return (row_data.astype(jnp.float32) + mixed).astype(jnp.bfloat16)


def feed_forward(row_data, w_up, w_down):
    hidden = jax.nn.gelu(
        jnp.dot(normalize(row_data), w_up, preferred_element_type=jnp.float32), approximate=True
    ).astype(jnp.bfloat16)
    return (
        row_data.astype(jnp.float32) + jnp.dot(hidden, w_down, preferred_element_type=jnp.float32)
    ).astype(jnp.bfloat16)


def place(onehot, rows):
    return jnp.dot(onehot, rows, preferred_element_type=jnp.float32).astype(jnp.bfloat16)


def place_back(onehot, rows):
    return lax.dot_general(
        onehot, rows, (((0,), (0,)), ((), ())), preferred_element_type=jnp.float32
    ).astype(jnp.bfloat16)


def on_device(points, rank, counts, w_qkv_one, w_out_one, w_up, w_down, w_qkv_two, w_out_two):
    owner_count = lax.axis_size("win")
    group_count = lax.axis_size("grp")
    win_index = lax.axis_index("win")
    grp_index = lax.axis_index("grp")
    local_points = points.shape[2]
    model_dim = points.shape[3]
    blocks = counts.shape[2]
    slots_all = blocks * WINDOW_SLOTS
    capacity = 2 * local_points // owner_count
    buffer_rows = owner_count * capacity
    dilation_stride = WINDOW_SLOTS // group_count
    rows_x = points.reshape(local_points, model_dim)
    point_rank = rank.reshape(local_points)
    column_counts = lax.dynamic_index_in_dim(counts, grp_index, 0, keepdims=False)

    owner_dev = point_rank // local_points
    owner_ids = jnp.arange(owner_count, dtype=jnp.int32)
    choose = (owner_dev[:, None] == owner_ids[None, :]).astype(jnp.int32)
    peer_order = jnp.sum(choose * (jnp.cumsum(choose, axis=0) - 1), axis=1)
    send_place = owner_dev * capacity + peer_order
    buffer_ids = jnp.arange(buffer_rows, dtype=jnp.int32)
    send_hot = (buffer_ids[:, None] == send_place[None, :]).astype(jnp.bfloat16)

    window_ends = jnp.cumsum(column_counts, axis=1)
    starts = window_ends - column_counts
    offset = point_rank % local_points
    owner_ends = jnp.sum(choose[:, :, None] * window_ends[None], axis=1)
    owner_starts = jnp.sum(choose[:, :, None] * starts[None], axis=1)
    window = jnp.sum((owner_ends <= offset[:, None]).astype(jnp.int32), axis=1)
    block_ids = jnp.arange(blocks, dtype=jnp.int32)
    block_pick = (window[:, None] == block_ids[None, :]).astype(jnp.int32)
    dest_slot = window * WINDOW_SLOTS + offset - jnp.sum(block_pick * owner_starts, axis=1)
    slot_code = dest_slot + 1
    tail_ids = jnp.arange(TAIL, dtype=jnp.int32)
    code_cols = jnp.where(
        tail_ids[None, :] == 0,
        (slot_code // SLOT_BASE)[:, None],
        jnp.where(tail_ids[None, :] == 1, (slot_code % SLOT_BASE)[:, None], 0),
    ).astype(jnp.bfloat16)
    outgoing = place(send_hot, jnp.concatenate([rows_x, code_cols], axis=1))
    receiving = lax.all_to_all(
        outgoing.reshape(owner_count, capacity, model_dim + TAIL),
        "win",
        split_axis=0,
        concat_axis=0,
        tiled=True,
    ).reshape(buffer_rows, model_dim + TAIL)
    arrived = receiving[:, :model_dim]
    code_back = receiving[:, model_dim:].astype(jnp.int32)
    arrived_slot = code_back[:, 0] * SLOT_BASE + code_back[:, 1] - 1
    own_counts = lax.dynamic_index_in_dim(column_counts, win_index, 0, keepdims=False)
    slot_ids = jnp.arange(slots_all, dtype=jnp.int32)
    recv_hot = (slot_ids[:, None] == arrived_slot.reshape(1, buffer_rows)).astype(jnp.bfloat16)
    padded_x = place(recv_hot, arrived)

    column = jnp.arange(WINDOW_SLOTS, dtype=jnp.int32)
    usable_mask = column[None, :] < own_counts[:, None]
    first_pad = feed_forward(attention_block(padded_x, usable_mask, w_qkv_one, w_out_one), w_up, w_down)
    dilated_rows = lax.all_to_all(
        first_pad.reshape(blocks, dilation_stride, group_count, model_dim),
        "grp",
        split_axis=2,
        concat_axis=1,
        tiled=True,
    )
    owner_counts = lax.dynamic_index_in_dim(counts, win_index, 1, keepdims=False)
    k_ids = jnp.arange(dilation_stride, dtype=jnp.int32)
    valid_marks = (k_ids[None, None, :] * group_count + grp_index) < jnp.transpose(owner_counts)[
        :, :, None
    ]
    block_count = dilated_rows.shape[0]
    flat_rows = dilated_rows.reshape(block_count * WINDOW_SLOTS, model_dim)
    mixed_rows = attention_block(
        flat_rows, valid_marks.reshape(block_count, WINDOW_SLOTS), w_qkv_two, w_out_two
    ).reshape(
        block_count, WINDOW_SLOTS, 1, model_dim
    )
    second_pad = lax.all_to_all(mixed_rows, "grp", split_axis=1, concat_axis=2, tiled=True).reshape(
        slots_all, model_dim
    )
    returning = place_back(recv_hot, second_pad)
    returned = lax.all_to_all(returning, "win", split_axis=0, concat_axis=0, tiled=True)
    encoded = place_back(send_hot, returned)
    return encoded.reshape(1, 1, local_points, model_dim)


def solution(mesh):
    return jax.shard_map(
        on_device,
        mesh=mesh,
        in_specs=(
            P("win", "grp", None, None),
            P("win", "grp", None),
            P(),
            P(),
            P(),
            P(),
            P(),
            P(),
            P(),
        ),
        out_specs=P("win", "grp", None, None),
        check_vma=False,
    )
```

```python
import jax
import jax.numpy as jnp
from jax import lax
from jax.sharding import Mesh, PartitionSpec as P

HEAD_DIM = 32
WINDOW_SLOTS = 128


EPSILON = 1e-05
MASKED = -1e30
WIN_SLOW = 4
SLOT_BASE = 32
TAIL = 128


def normalize(row_data):
    values = row_data.astype(jnp.float32)
    center = values - jnp.mean(values, axis=-1, keepdims=True)
    spread = jnp.mean(center * center, axis=-1, keepdims=True)
    return (center * lax.rsqrt(spread + EPSILON)).astype(jnp.bfloat16)


def project(row_data, weight):
    return jnp.dot(normalize(row_data), weight, preferred_element_type=jnp.float32).astype(
        jnp.bfloat16
    )


def attention_block(row_data, valid, w_qkv, w_out):
    rows_count, model_dim = row_data.shape
    heads_count = model_dim // HEAD_DIM
    block_count = rows_count // WINDOW_SLOTS
    normed = normalize(row_data)
    w_split = w_qkv.reshape(model_dim, 3, heads_count, HEAD_DIM)

    def head_major(part):
        out = jnp.einsum("nd,dhe->hne", normed, w_split[:, part], preferred_element_type=jnp.float32)
        return out.astype(jnp.bfloat16).reshape(heads_count, block_count, WINDOW_SLOTS, HEAD_DIM)

    query, key, value = head_major(0), head_major(1), head_major(2)
    scores = jnp.einsum(
        "hbqe,hbke->hbqk", query, key, preferred_element_type=jnp.float32
    ) * HEAD_DIM ** (-0.5)
    scores = jnp.where(valid[None, :, None, :], scores, MASKED)
    row_max = jnp.max(scores, axis=-1, keepdims=True)
    weights = jnp.exp(scores - row_max)
    weights = (weights / jnp.sum(weights, axis=-1, keepdims=True)).astype(jnp.bfloat16)
    context = jnp.einsum("hbqk,hbke->hbqe", weights, value, preferred_element_type=jnp.float32)
    context = context.astype(jnp.bfloat16).reshape(heads_count, rows_count, HEAD_DIM)
    mixed = jnp.einsum(
        "hne,hed->nd",
        context,
        w_out.reshape(heads_count, HEAD_DIM, model_dim),
        preferred_element_type=jnp.float32,
    )
    return (row_data.astype(jnp.float32) + mixed).astype(jnp.bfloat16)


def feed_forward(row_data, w_up, w_down):
    hidden = jax.nn.gelu(
        jnp.dot(normalize(row_data), w_up, preferred_element_type=jnp.float32), approximate=True
    ).astype(jnp.bfloat16)
    return (
        row_data.astype(jnp.float32) + jnp.dot(hidden, w_down, preferred_element_type=jnp.float32)
    ).astype(jnp.bfloat16)


def place(onehot, rows):
    return jnp.dot(onehot, rows, preferred_element_type=jnp.float32).astype(jnp.bfloat16)


def place_back(onehot, rows):
    return lax.dot_general(
        onehot, rows, (((0,), (0,)), ((), ())), preferred_element_type=jnp.float32
    ).astype(jnp.bfloat16)


def exchange_win(rows, capacity):
    slow, fast = lax.axis_size("win_slow"), lax.axis_size("win_fast")
    blocks = rows.reshape(slow, fast, capacity, rows.shape[-1])
    blocks = lax.all_to_all(blocks, "win_fast", split_axis=1, concat_axis=1, tiled=True)
    return lax.all_to_all(blocks, "win_slow", split_axis=0, concat_axis=0, tiled=True)


def on_device(points, rank, counts, w_qkv_one, w_out_one, w_up, w_down, w_qkv_two, w_out_two):
    owner_count = lax.axis_size("win_slow") * lax.axis_size("win_fast")
    group_count = lax.axis_size("grp")
    win_index = lax.axis_index("win_slow") * lax.axis_size("win_fast") + lax.axis_index("win_fast")
    grp_index = lax.axis_index("grp")
    local_points = points.shape[2]
    model_dim = points.shape[3]
    blocks = counts.shape[2]
    slots_all = blocks * WINDOW_SLOTS
    capacity = 2 * local_points // owner_count
    buffer_rows = owner_count * capacity
    dilation_stride = WINDOW_SLOTS // group_count
    rows_x = points.reshape(local_points, model_dim)
    point_rank = rank.reshape(local_points)
    column_counts = lax.dynamic_index_in_dim(counts, grp_index, 0, keepdims=False)

    owner_dev = point_rank // local_points
    owner_ids = jnp.arange(owner_count, dtype=jnp.int32)
    choose = (owner_dev[:, None] == owner_ids[None, :]).astype(jnp.int32)
    peer_order = jnp.sum(choose * (jnp.cumsum(choose, axis=0) - 1), axis=1)
    send_place = owner_dev * capacity + peer_order
    buffer_ids = jnp.arange(buffer_rows, dtype=jnp.int32)
    send_hot = (buffer_ids[:, None] == send_place[None, :]).astype(jnp.bfloat16)

    window_ends = jnp.cumsum(column_counts, axis=1)
    starts = window_ends - column_counts
    offset = point_rank % local_points
    owner_ends = jnp.sum(choose[:, :, None] * window_ends[None], axis=1)
    owner_starts = jnp.sum(choose[:, :, None] * starts[None], axis=1)
    window = jnp.sum((owner_ends <= offset[:, None]).astype(jnp.int32), axis=1)
    block_ids = jnp.arange(blocks, dtype=jnp.int32)
    block_pick = (window[:, None] == block_ids[None, :]).astype(jnp.int32)
    dest_slot = window * WINDOW_SLOTS + offset - jnp.sum(block_pick * owner_starts, axis=1)
    slot_code = dest_slot + 1
    tail_ids = jnp.arange(TAIL, dtype=jnp.int32)
    code_cols = jnp.where(
        tail_ids[None, :] == 0,
        (slot_code // SLOT_BASE)[:, None],
        jnp.where(tail_ids[None, :] == 1, (slot_code % SLOT_BASE)[:, None], 0),
    ).astype(jnp.bfloat16)
    outgoing = place(send_hot, jnp.concatenate([rows_x, code_cols], axis=1))
    receiving = exchange_win(outgoing, capacity).reshape(buffer_rows, model_dim + TAIL)
    arrived = receiving[:, :model_dim]
    code_back = receiving[:, model_dim:].astype(jnp.int32)
    arrived_slot = code_back[:, 0] * SLOT_BASE + code_back[:, 1] - 1
    own_counts = lax.dynamic_index_in_dim(column_counts, win_index, 0, keepdims=False)
    slot_ids = jnp.arange(slots_all, dtype=jnp.int32)
    recv_hot = (slot_ids[:, None] == arrived_slot.reshape(1, buffer_rows)).astype(jnp.bfloat16)
    padded_x = place(recv_hot, arrived)

    column = jnp.arange(WINDOW_SLOTS, dtype=jnp.int32)
    usable_mask = column[None, :] < own_counts[:, None]
    first_pad = feed_forward(attention_block(padded_x, usable_mask, w_qkv_one, w_out_one), w_up, w_down)
    dilated_rows = lax.all_to_all(
        first_pad.reshape(blocks, dilation_stride, group_count, model_dim),
        "grp",
        split_axis=2,
        concat_axis=1,
        tiled=True,
    )
    owner_counts = lax.dynamic_index_in_dim(counts, win_index, 1, keepdims=False)
    k_ids = jnp.arange(dilation_stride, dtype=jnp.int32)
    valid_marks = (k_ids[None, None, :] * group_count + grp_index) < jnp.transpose(owner_counts)[
        :, :, None
    ]
    block_count = dilated_rows.shape[0]
    flat_rows = dilated_rows.reshape(block_count * WINDOW_SLOTS, model_dim)
    mixed_rows = attention_block(
        flat_rows, valid_marks.reshape(block_count, WINDOW_SLOTS), w_qkv_two, w_out_two
    ).reshape(
        block_count, WINDOW_SLOTS, 1, model_dim
    )
    second_pad = lax.all_to_all(mixed_rows, "grp", split_axis=1, concat_axis=2, tiled=True).reshape(
        slots_all, model_dim
    )
    returning = place_back(recv_hot, second_pad)
    returned = exchange_win(returning, capacity).reshape(buffer_rows, model_dim)
    encoded = place_back(send_hot, returned)
    return encoded.reshape(1, 1, local_points, model_dim)


def solution(mesh):
    devices = mesh.devices
    slow = WIN_SLOW
    split_mesh = Mesh(
        devices.reshape(slow, devices.shape[0] // slow, devices.shape[1]),
        ("win_slow", "win_fast", "grp"),
    )
    win = ("win_slow", "win_fast")
    return jax.shard_map(
        on_device,
        mesh=split_mesh,
        in_specs=(
            P(win, "grp", None, None),
            P(win, "grp", None),
            P(),
            P(),
            P(),
            P(),
            P(),
            P(),
            P(),
        ),
        out_specs=P(win, "grp", None, None),
        check_vma=False,
    )
```

```python
import jax
import jax.numpy as jnp
from jax import lax
from jax.sharding import PartitionSpec as P

HEAD_DIM = 32
WINDOW_SLOTS = 128


EPSILON = 1e-05
MASKED = -1e30
SLOT_BASE = 32
TAIL = 128


def normalize(row_data):
    values = row_data.astype(jnp.float32)
    center = values - jnp.mean(values, axis=-1, keepdims=True)
    spread = jnp.mean(center * center, axis=-1, keepdims=True)
    return (center * lax.rsqrt(spread + EPSILON)).astype(jnp.bfloat16)


def project(row_data, weight):
    return jnp.dot(normalize(row_data), weight, preferred_element_type=jnp.float32).astype(
        jnp.bfloat16
    )


def attention_block(row_data, valid, w_qkv, w_out):
    rows_count, model_dim = row_data.shape
    heads_count = model_dim // HEAD_DIM
    block_count = rows_count // WINDOW_SLOTS
    normed = normalize(row_data)
    w_split = w_qkv.reshape(model_dim, 3, heads_count, HEAD_DIM)

    def head_major(part):
        out = jnp.einsum("nd,dhe->hne", normed, w_split[:, part], preferred_element_type=jnp.float32)
        return out.astype(jnp.bfloat16).reshape(heads_count, block_count, WINDOW_SLOTS, HEAD_DIM)

    query, key, value = head_major(0), head_major(1), head_major(2)
    scores = jnp.einsum(
        "hbqe,hbke->hbqk", query, key, preferred_element_type=jnp.float32
    ) * HEAD_DIM ** (-0.5)
    scores = jnp.where(valid[None, :, None, :], scores, MASKED)
    row_max = jnp.max(scores, axis=-1, keepdims=True)
    weights = jnp.exp(scores - row_max)
    weights = (weights / jnp.sum(weights, axis=-1, keepdims=True)).astype(jnp.bfloat16)
    context = jnp.einsum("hbqk,hbke->hbqe", weights, value, preferred_element_type=jnp.float32)
    context = context.astype(jnp.bfloat16).reshape(heads_count, rows_count, HEAD_DIM)
    mixed = jnp.einsum(
        "hne,hed->nd",
        context,
        w_out.reshape(heads_count, HEAD_DIM, model_dim),
        preferred_element_type=jnp.float32,
    )
    return (row_data.astype(jnp.float32) + mixed).astype(jnp.bfloat16)


def feed_forward(row_data, w_up, w_down):
    hidden = jax.nn.gelu(
        jnp.dot(normalize(row_data), w_up, preferred_element_type=jnp.float32), approximate=True
    ).astype(jnp.bfloat16)
    return (
        row_data.astype(jnp.float32) + jnp.dot(hidden, w_down, preferred_element_type=jnp.float32)
    ).astype(jnp.bfloat16)


def place(onehot, rows):
    return jnp.dot(onehot, rows, preferred_element_type=jnp.float32).astype(jnp.bfloat16)


def place_back(onehot, rows):
    return lax.dot_general(
        onehot, rows, (((0,), (0,)), ((), ())), preferred_element_type=jnp.float32
    ).astype(jnp.bfloat16)


def on_device(points, rank, counts, w_qkv_one, w_out_one, w_up, w_down, w_qkv_two, w_out_two):
    owner_count = lax.axis_size("win")
    group_count = lax.axis_size("grp")
    win_index = lax.axis_index("win")
    grp_index = lax.axis_index("grp")
    local_points = points.shape[2]
    model_dim = points.shape[3]
    blocks = counts.shape[2]
    slots_all = blocks * WINDOW_SLOTS
    capacity = 2 * local_points // owner_count
    buffer_rows = owner_count * capacity
    dilation_stride = WINDOW_SLOTS // group_count
    rows_x = points.reshape(local_points, model_dim)
    point_rank = rank.reshape(local_points)
    column_counts = lax.dynamic_index_in_dim(counts, grp_index, 0, keepdims=False)

    owner_dev = point_rank // local_points
    owner_ids = jnp.arange(owner_count, dtype=jnp.int32)
    choose = (owner_dev[:, None] == owner_ids[None, :]).astype(jnp.int32)
    peer_order = jnp.sum(choose * (jnp.cumsum(choose, axis=0) - 1), axis=1)
    send_place = owner_dev * capacity + peer_order
    buffer_ids = jnp.arange(buffer_rows, dtype=jnp.int32)
    send_hot = (buffer_ids[:, None] == send_place[None, :]).astype(jnp.bfloat16)

    window_ends = jnp.cumsum(column_counts, axis=1)
    starts = window_ends - column_counts
    offset = point_rank % local_points
    owner_ends = jnp.sum(choose[:, :, None] * window_ends[None], axis=1)
    owner_starts = jnp.sum(choose[:, :, None] * starts[None], axis=1)
    window = jnp.sum((owner_ends <= offset[:, None]).astype(jnp.int32), axis=1)
    block_ids = jnp.arange(blocks, dtype=jnp.int32)
    block_pick = (window[:, None] == block_ids[None, :]).astype(jnp.int32)
    dest_slot = window * WINDOW_SLOTS + offset - jnp.sum(block_pick * owner_starts, axis=1)
    slot_code = dest_slot + 1
    tail_ids = jnp.arange(TAIL, dtype=jnp.int32)
    code_cols = jnp.where(
        tail_ids[None, :] == 0,
        (slot_code // SLOT_BASE)[:, None],
        jnp.where(tail_ids[None, :] == 1, (slot_code % SLOT_BASE)[:, None], 0),
    ).astype(jnp.bfloat16)
    outgoing = place(send_hot, jnp.concatenate([rows_x, code_cols], axis=1))
    receiving = lax.all_to_all(
        outgoing.reshape(owner_count, capacity, model_dim + TAIL),
        "win",
        split_axis=0,
        concat_axis=0,
        tiled=True,
    ).reshape(buffer_rows, model_dim + TAIL)
    arrived = receiving[:, :model_dim]
    code_back = receiving[:, model_dim:].astype(jnp.int32)
    arrived_slot = code_back[:, 0] * SLOT_BASE + code_back[:, 1] - 1
    own_counts = lax.dynamic_index_in_dim(column_counts, win_index, 0, keepdims=False)
    slot_ids = jnp.arange(slots_all, dtype=jnp.int32)
    recv_hot = (slot_ids[:, None] == arrived_slot.reshape(1, buffer_rows)).astype(jnp.bfloat16)
    padded_x = place(recv_hot, arrived)

    column = jnp.arange(WINDOW_SLOTS, dtype=jnp.int32)
    usable_mask = column[None, :] < own_counts[:, None]
    first_pad = feed_forward(attention_block(padded_x, usable_mask, w_qkv_one, w_out_one), w_up, w_down)
    dilated_rows = lax.all_to_all(
        first_pad.reshape(blocks, dilation_stride, group_count, model_dim),
        "grp",
        split_axis=2,
        concat_axis=1,
        tiled=True,
    )
    owner_counts = lax.dynamic_index_in_dim(counts, win_index, 1, keepdims=False)
    k_ids = jnp.arange(dilation_stride, dtype=jnp.int32)
    valid_marks = (k_ids[None, None, :] * group_count + grp_index) < jnp.transpose(owner_counts)[
        :, :, None
    ]
    block_count = dilated_rows.shape[0]
    flat_rows = dilated_rows.reshape(block_count * WINDOW_SLOTS, model_dim)
    mixed_rows = attention_block(
        flat_rows, valid_marks.reshape(block_count, WINDOW_SLOTS), w_qkv_two, w_out_two
    )
    mixed_rows = jnp.transpose(mixed_rows.reshape(block_count, WINDOW_SLOTS, model_dim), (1, 0, 2))
    second_pad = lax.all_to_all(
        mixed_rows.reshape(WINDOW_SLOTS, block_count, 1, model_dim),
        "grp",
        split_axis=0,
        concat_axis=2,
        tiled=True,
    ).reshape(slots_all, model_dim)
    row_ids = jnp.arange(slots_all, dtype=jnp.int32)
    row_k = row_ids // (blocks * group_count)
    row_b = (row_ids // group_count) % blocks
    row_r = row_ids % group_count
    row_slot = row_b * WINDOW_SLOTS + row_k * group_count + row_r
    back_hot = (row_slot[:, None] == arrived_slot.reshape(1, buffer_rows)).astype(jnp.bfloat16)
    returning = place_back(back_hot, second_pad)
    returned = lax.all_to_all(returning, "win", split_axis=0, concat_axis=0, tiled=True)
    encoded = place_back(send_hot, returned)
    return encoded.reshape(1, 1, local_points, model_dim)


def solution(mesh):
    return jax.shard_map(
        on_device,
        mesh=mesh,
        in_specs=(
            P("win", "grp", None, None),
            P("win", "grp", None),
            P(),
            P(),
            P(),
            P(),
            P(),
            P(),
            P(),
        ),
        out_specs=P("win", "grp", None, None),
        check_vma=False,
    )
```

```python
import jax
import jax.numpy as jnp
from jax import lax
from jax.sharding import PartitionSpec as P

HEAD_DIM = 32
WINDOW_SLOTS = 128


EPSILON = 1e-05
MASKED = -1e30
SLOT_BASE = 32
TAIL = 128


def normalize(row_data):
    values = row_data.astype(jnp.float32)
    center = values - jnp.mean(values, axis=-1, keepdims=True)
    spread = jnp.mean(center * center, axis=-1, keepdims=True)
    return (center * lax.rsqrt(spread + EPSILON)).astype(jnp.bfloat16)


def project(row_data, weight):
    return jnp.dot(normalize(row_data), weight, preferred_element_type=jnp.float32).astype(
        jnp.bfloat16
    )


def attention_block(row_data, valid, w_qkv, w_out):
    rows_count, model_dim = row_data.shape
    heads_count = model_dim // HEAD_DIM
    block_count = rows_count // WINDOW_SLOTS
    normed = normalize(row_data)
    w_split = w_qkv.reshape(model_dim, 3, heads_count, HEAD_DIM)

    def head_major(part):
        out = jnp.einsum("nd,dhe->hne", normed, w_split[:, part], preferred_element_type=jnp.float32)
        return out.astype(jnp.bfloat16).reshape(heads_count, block_count, WINDOW_SLOTS, HEAD_DIM)

    query, key, value = head_major(0), head_major(1), head_major(2)
    scores = jnp.einsum(
        "hbqe,hbke->hbqk", query, key, preferred_element_type=jnp.float32
    ) * HEAD_DIM ** (-0.5)
    scores = jnp.where(valid[None, :, None, :], scores, MASKED)
    row_max = jnp.max(scores, axis=-1, keepdims=True)
    weights = jnp.exp(scores - row_max)
    weights = (weights / jnp.sum(weights, axis=-1, keepdims=True)).astype(jnp.bfloat16)
    context = jnp.einsum("hbqk,hbke->hbqe", weights, value, preferred_element_type=jnp.float32)
    context = context.astype(jnp.bfloat16).reshape(heads_count, rows_count, HEAD_DIM)
    mixed = jnp.einsum(
        "hne,hed->nd",
        context,
        w_out.reshape(heads_count, HEAD_DIM, model_dim),
        preferred_element_type=jnp.float32,
    )
    return (row_data.astype(jnp.float32) + mixed).astype(jnp.bfloat16)


def feed_forward(row_data, w_up, w_down):
    hidden = jax.nn.gelu(
        jnp.dot(normalize(row_data), w_up, preferred_element_type=jnp.float32), approximate=True
    ).astype(jnp.bfloat16)
    return (
        row_data.astype(jnp.float32) + jnp.dot(hidden, w_down, preferred_element_type=jnp.float32)
    ).astype(jnp.bfloat16)


def place(onehot, rows):
    return jnp.dot(onehot, rows, preferred_element_type=jnp.float32).astype(jnp.bfloat16)


def place_back(onehot, rows):
    return lax.dot_general(
        onehot, rows, (((0,), (0,)), ((), ())), preferred_element_type=jnp.float32
    ).astype(jnp.bfloat16)


def on_device(points, rank, counts, w_qkv_one, w_out_one, w_up, w_down, w_qkv_two, w_out_two):
    owner_count = lax.axis_size("win")
    group_count = lax.axis_size("grp")
    win_index = lax.axis_index("win")
    grp_index = lax.axis_index("grp")
    local_points = points.shape[2]
    model_dim = points.shape[3]
    blocks = counts.shape[2]
    slots_all = blocks * WINDOW_SLOTS
    capacity = 2 * local_points // owner_count
    buffer_rows = owner_count * capacity
    dilation_stride = WINDOW_SLOTS // group_count
    rows_x = points.reshape(local_points, model_dim)
    point_rank = rank.reshape(local_points)
    column_counts = lax.dynamic_index_in_dim(counts, grp_index, 0, keepdims=False)

    owner_dev = point_rank // local_points
    owner_ids = jnp.arange(owner_count, dtype=jnp.int32)
    choose = (owner_dev[:, None] == owner_ids[None, :]).astype(jnp.int32)
    peer_order = jnp.sum(choose * (jnp.cumsum(choose, axis=0) - 1), axis=1)
    send_place = owner_dev * capacity + peer_order
    buffer_ids = jnp.arange(buffer_rows, dtype=jnp.int32)
    send_hot = (buffer_ids[:, None] == send_place[None, :]).astype(jnp.bfloat16)

    window_ends = jnp.cumsum(column_counts, axis=1)
    starts = window_ends - column_counts
    offset = point_rank % local_points
    owner_ends = jnp.sum(choose[:, :, None] * window_ends[None], axis=1)
    owner_starts = jnp.sum(choose[:, :, None] * starts[None], axis=1)
    window = jnp.sum((owner_ends <= offset[:, None]).astype(jnp.int32), axis=1)
    block_ids = jnp.arange(blocks, dtype=jnp.int32)
    block_pick = (window[:, None] == block_ids[None, :]).astype(jnp.int32)
    dest_slot = window * WINDOW_SLOTS + offset - jnp.sum(block_pick * owner_starts, axis=1)
    slot_code = dest_slot + 1
    tail_ids = jnp.arange(TAIL, dtype=jnp.int32)
    code_cols = jnp.where(
        tail_ids[None, :] == 0,
        (slot_code // SLOT_BASE)[:, None],
        jnp.where(tail_ids[None, :] == 1, (slot_code % SLOT_BASE)[:, None], 0),
    ).astype(jnp.bfloat16)
    outgoing = place(send_hot, jnp.concatenate([rows_x, code_cols], axis=1))
    receiving = lax.all_to_all(
        outgoing.reshape(owner_count, capacity, model_dim + TAIL),
        "win",
        split_axis=0,
        concat_axis=0,
        tiled=True,
    ).reshape(buffer_rows, model_dim + TAIL)
    arrived = receiving[:, :model_dim]
    code_back = receiving[:, model_dim:].astype(jnp.int32)
    arrived_slot = code_back[:, 0] * SLOT_BASE + code_back[:, 1] - 1
    own_counts = lax.dynamic_index_in_dim(column_counts, win_index, 0, keepdims=False)
    slot_ids = jnp.arange(slots_all, dtype=jnp.int32)
    recv_hot = (slot_ids[:, None] == arrived_slot.reshape(1, buffer_rows)).astype(jnp.bfloat16)
    padded_x = place(recv_hot, arrived)

    column = jnp.arange(WINDOW_SLOTS, dtype=jnp.int32)
    usable_mask = column[None, :] < own_counts[:, None]
    first_mixed = attention_block(padded_x, usable_mask, w_qkv_one, w_out_one)
    row_ids = jnp.arange(slots_all, dtype=jnp.int32)
    row_r = row_ids // (blocks * dilation_stride)
    row_b = (row_ids // dilation_stride) % blocks
    row_k = row_ids % dilation_stride
    source_row = row_b * WINDOW_SLOTS + row_k * group_count + row_r
    order_hot = (source_row[:, None] == row_ids[None, :]).astype(jnp.bfloat16)
    first_pad = feed_forward(place(order_hot, first_mixed), w_up, w_down)
    dilated_rows = lax.all_to_all(
        first_pad.reshape(group_count, blocks, dilation_stride, model_dim),
        "grp",
        split_axis=0,
        concat_axis=2,
        tiled=True,
    )
    block_count = blocks
    owner_counts = lax.dynamic_index_in_dim(counts, win_index, 1, keepdims=False)
    k_ids = jnp.arange(dilation_stride, dtype=jnp.int32)
    valid_marks = (k_ids[None, None, :] * group_count + grp_index) < jnp.transpose(owner_counts)[
        :, :, None
    ]
    flat_rows = dilated_rows.reshape(block_count * WINDOW_SLOTS, model_dim)
    mixed_rows = attention_block(
        flat_rows, valid_marks.reshape(block_count, WINDOW_SLOTS), w_qkv_two, w_out_two
    ).reshape(
        block_count, WINDOW_SLOTS, 1, model_dim
    )
    second_pad = lax.all_to_all(mixed_rows, "grp", split_axis=1, concat_axis=2, tiled=True).reshape(
        slots_all, model_dim
    )
    returning = place_back(recv_hot, second_pad)
    returned = lax.all_to_all(returning, "win", split_axis=0, concat_axis=0, tiled=True)
    encoded = place_back(send_hot, returned)
    return encoded.reshape(1, 1, local_points, model_dim)


def solution(mesh):
    return jax.shard_map(
        on_device,
        mesh=mesh,
        in_specs=(
            P("win", "grp", None, None),
            P("win", "grp", None),
            P(),
            P(),
            P(),
            P(),
            P(),
            P(),
            P(),
        ),
        out_specs=P("win", "grp", None, None),
        check_vma=False,
    )
```

```python
import jax
import jax.numpy as jnp
from jax import lax
from jax.sharding import PartitionSpec as P

HEAD_DIM = 32
WINDOW_SLOTS = 128


EPSILON = 1e-05
MASKED = -1e30
SLOT_BASE = 32
TAIL = 128


def normalize(row_data):
    values = row_data.astype(jnp.float32)
    center = values - jnp.mean(values, axis=-1, keepdims=True)
    spread = jnp.mean(center * center, axis=-1, keepdims=True)
    return (center * lax.rsqrt(spread + EPSILON)).astype(jnp.bfloat16)


def project(row_data, weight):
    return jnp.dot(normalize(row_data), weight, preferred_element_type=jnp.float32).astype(
        jnp.bfloat16
    )


def attention_block(row_data, valid, w_qkv, w_out):
    rows_count, model_dim = row_data.shape
    heads_count = model_dim // HEAD_DIM
    block_count = rows_count // WINDOW_SLOTS
    normed = normalize(row_data)
    w_split = w_qkv.reshape(model_dim, 3, heads_count, HEAD_DIM)

    def head_major(part):
        out = jnp.einsum("nd,dhe->hne", normed, w_split[:, part], preferred_element_type=jnp.float32)
        return out.astype(jnp.bfloat16).reshape(heads_count, block_count, WINDOW_SLOTS, HEAD_DIM)

    query, key, value = head_major(0), head_major(1), head_major(2)
    scores = jnp.einsum(
        "hbqe,hbke->hbqk", query, key, preferred_element_type=jnp.float32
    ) * HEAD_DIM ** (-0.5)
    scores = jnp.where(valid[None, :, None, :], scores, MASKED)
    row_max = jnp.max(scores, axis=-1, keepdims=True)
    weights = jnp.exp(scores - row_max)
    weights = (weights / jnp.sum(weights, axis=-1, keepdims=True)).astype(jnp.bfloat16)
    context = jnp.einsum("hbqk,hbke->hbqe", weights, value, preferred_element_type=jnp.float32)
    context = context.astype(jnp.bfloat16).reshape(heads_count, rows_count, HEAD_DIM)
    mixed = jnp.einsum(
        "hne,hed->nd",
        context,
        w_out.reshape(heads_count, HEAD_DIM, model_dim),
        preferred_element_type=jnp.float32,
    )
    return (row_data.astype(jnp.float32) + mixed).astype(jnp.bfloat16)


def feed_forward(row_data, w_up, w_down):
    hidden = jax.nn.gelu(
        jnp.dot(normalize(row_data), w_up, preferred_element_type=jnp.float32), approximate=True
    ).astype(jnp.bfloat16)
    return (
        row_data.astype(jnp.float32) + jnp.dot(hidden, w_down, preferred_element_type=jnp.float32)
    ).astype(jnp.bfloat16)


def place(onehot, rows):
    return jnp.dot(onehot, rows, preferred_element_type=jnp.float32).astype(jnp.bfloat16)


def place_back(onehot, rows):
    return lax.dot_general(
        onehot, rows, (((0,), (0,)), ((), ())), preferred_element_type=jnp.float32
    ).astype(jnp.bfloat16)


def on_device(points, rank, counts, w_qkv_one, w_out_one, w_up, w_down, w_qkv_two, w_out_two):
    owner_count = lax.axis_size("win")
    group_count = lax.axis_size("grp")
    win_index = lax.axis_index("win")
    grp_index = lax.axis_index("grp")
    local_points = points.shape[2]
    model_dim = points.shape[3]
    blocks = counts.shape[2]
    slots_all = blocks * WINDOW_SLOTS
    capacity = 2 * local_points // owner_count
    buffer_rows = owner_count * capacity
    dilation_stride = WINDOW_SLOTS // group_count
    rows_x = points.reshape(local_points, model_dim)
    point_rank = rank.reshape(local_points)
    column_counts = lax.dynamic_index_in_dim(counts, grp_index, 0, keepdims=False)

    owner_dev = point_rank // local_points
    owner_ids = jnp.arange(owner_count, dtype=jnp.int32)
    choose = (owner_dev[:, None] == owner_ids[None, :]).astype(jnp.int32)
    point_ids = jnp.arange(local_points, dtype=jnp.int32)
    lower = (point_ids[None, :] <= point_ids[:, None]).astype(jnp.bfloat16)
    running = jnp.dot(lower, choose.astype(jnp.bfloat16), preferred_element_type=jnp.float32)
    peer_order = jnp.sum(choose * (running.astype(jnp.int32) - 1), axis=1)
    send_place = owner_dev * capacity + peer_order
    buffer_ids = jnp.arange(buffer_rows, dtype=jnp.int32)
    send_hot = (buffer_ids[:, None] == send_place[None, :]).astype(jnp.bfloat16)

    window_ends = jnp.cumsum(column_counts, axis=1)
    starts = window_ends - column_counts
    offset = point_rank % local_points
    table = jnp.concatenate(
        [window_ends // SLOT_BASE, window_ends % SLOT_BASE, starts // SLOT_BASE, starts % SLOT_BASE], axis=1
    ).astype(jnp.bfloat16)
    picked = jnp.dot(choose.astype(jnp.bfloat16), table, preferred_element_type=jnp.float32)
    picked = picked.astype(jnp.int32)
    owner_ends = picked[:, :blocks] * SLOT_BASE + picked[:, blocks : 2 * blocks]
    owner_starts = picked[:, 2 * blocks : 3 * blocks] * SLOT_BASE + picked[:, 3 * blocks :]
    window = jnp.sum((owner_ends <= offset[:, None]).astype(jnp.int32), axis=1)
    block_ids = jnp.arange(blocks, dtype=jnp.int32)
    block_pick = (window[:, None] == block_ids[None, :]).astype(jnp.int32)
    dest_slot = window * WINDOW_SLOTS + offset - jnp.sum(block_pick * owner_starts, axis=1)
    slot_code = dest_slot + 1
    tail_ids = jnp.arange(TAIL, dtype=jnp.int32)
    code_cols = jnp.where(
        tail_ids[None, :] == 0,
        (slot_code // SLOT_BASE)[:, None],
        jnp.where(tail_ids[None, :] == 1, (slot_code % SLOT_BASE)[:, None], 0),
    ).astype(jnp.bfloat16)
    outgoing = place(send_hot, jnp.concatenate([rows_x, code_cols], axis=1))
    receiving = lax.all_to_all(
        outgoing.reshape(owner_count, capacity, model_dim + TAIL),
        "win",
        split_axis=0,
        concat_axis=0,
        tiled=True,
    ).reshape(buffer_rows, model_dim + TAIL)
    arrived = receiving[:, :model_dim]
    code_back = receiving[:, model_dim:].astype(jnp.int32)
    arrived_slot = code_back[:, 0] * SLOT_BASE + code_back[:, 1] - 1
    own_counts = lax.dynamic_index_in_dim(column_counts, win_index, 0, keepdims=False)
    slot_ids = jnp.arange(slots_all, dtype=jnp.int32)
    recv_hot = (slot_ids[:, None] == arrived_slot.reshape(1, buffer_rows)).astype(jnp.bfloat16)
    padded_x = place(recv_hot, arrived)

    column = jnp.arange(WINDOW_SLOTS, dtype=jnp.int32)
    usable_mask = column[None, :] < own_counts[:, None]
    first_pad = feed_forward(attention_block(padded_x, usable_mask, w_qkv_one, w_out_one), w_up, w_down)
    dilated_rows = lax.all_to_all(
        first_pad.reshape(blocks, dilation_stride, group_count, model_dim),
        "grp",
        split_axis=2,
        concat_axis=1,
        tiled=True,
    )
    owner_counts = lax.dynamic_index_in_dim(counts, win_index, 1, keepdims=False)
    k_ids = jnp.arange(dilation_stride, dtype=jnp.int32)
    valid_marks = (k_ids[None, None, :] * group_count + grp_index) < jnp.transpose(owner_counts)[
        :, :, None
    ]
    block_count = dilated_rows.shape[0]
    flat_rows = dilated_rows.reshape(block_count * WINDOW_SLOTS, model_dim)
    mixed_rows = attention_block(
        flat_rows, valid_marks.reshape(block_count, WINDOW_SLOTS), w_qkv_two, w_out_two
    ).reshape(
        block_count, WINDOW_SLOTS, 1, model_dim
    )
    second_pad = lax.all_to_all(mixed_rows, "grp", split_axis=1, concat_axis=2, tiled=True).reshape(
        slots_all, model_dim
    )
    returning = place_back(recv_hot, second_pad)
    returned = lax.all_to_all(returning, "win", split_axis=0, concat_axis=0, tiled=True)
    encoded = place_back(send_hot, returned)
    return encoded.reshape(1, 1, local_points, model_dim)


def solution(mesh):
    return jax.shard_map(
        on_device,
        mesh=mesh,
        in_specs=(
            P("win", "grp", None, None),
            P("win", "grp", None),
            P(),
            P(),
            P(),
            P(),
            P(),
            P(),
            P(),
        ),
        out_specs=P("win", "grp", None, None),
        check_vma=False,
    )
```

```python
import jax
import jax.numpy as jnp
from jax import lax
from jax.sharding import PartitionSpec as P

HEAD_DIM = 32
WINDOW_SLOTS = 128


EPSILON = 1e-05
MASKED = -1e30
SLOT_BASE = 32
TAIL = 128


def normalize(row_data):
    values = row_data.astype(jnp.float32)
    center = values - jnp.mean(values, axis=-1, keepdims=True)
    spread = jnp.mean(center * center, axis=-1, keepdims=True)
    return (center * lax.rsqrt(spread + EPSILON)).astype(jnp.bfloat16)


def project(row_data, weight):
    return jnp.dot(normalize(row_data), weight, preferred_element_type=jnp.float32).astype(
        jnp.bfloat16
    )


def attention_block(row_data, valid, w_qkv, w_out):
    rows_count, model_dim = row_data.shape
    heads_count = model_dim // HEAD_DIM
    block_count = rows_count // WINDOW_SLOTS
    normed = normalize(row_data)
    w_split = w_qkv.reshape(model_dim, 3, heads_count, HEAD_DIM)

    def head_major(part):
        out = jnp.einsum("nd,dhe->hne", normed, w_split[:, part], preferred_element_type=jnp.float32)
        return out.astype(jnp.bfloat16).reshape(heads_count, block_count, WINDOW_SLOTS, HEAD_DIM)

    query, key, value = head_major(0), head_major(1), head_major(2)
    scores = jnp.einsum(
        "hbqe,hbke->hbqk", query, key, preferred_element_type=jnp.float32
    ) * HEAD_DIM ** (-0.5)
    scores = jnp.where(valid[None, :, None, :], scores, MASKED)
    row_max = jnp.max(scores, axis=-1, keepdims=True)
    weights = jnp.exp(scores - row_max)
    weights = (weights / jnp.sum(weights, axis=-1, keepdims=True)).astype(jnp.bfloat16)
    context = jnp.einsum("hbqk,hbke->hbqe", weights, value, preferred_element_type=jnp.float32)
    context = context.astype(jnp.bfloat16).reshape(heads_count, rows_count, HEAD_DIM)
    mixed = jnp.einsum(
        "hne,hed->nd",
        context,
        w_out.reshape(heads_count, HEAD_DIM, model_dim),
        preferred_element_type=jnp.float32,
    )
    return (row_data.astype(jnp.float32) + mixed).astype(jnp.bfloat16)


def feed_forward(row_data, w_up, w_down):
    hidden = jax.nn.gelu(
        jnp.dot(normalize(row_data), w_up, preferred_element_type=jnp.float32), approximate=True
    ).astype(jnp.bfloat16)
    return (
        row_data.astype(jnp.float32) + jnp.dot(hidden, w_down, preferred_element_type=jnp.float32)
    ).astype(jnp.bfloat16)


def place(onehot, rows):
    return jnp.dot(onehot, rows, preferred_element_type=jnp.float32).astype(jnp.bfloat16)


def place_back(onehot, rows):
    return lax.dot_general(
        onehot, rows, (((0,), (0,)), ((), ())), preferred_element_type=jnp.float32
    ).astype(jnp.bfloat16)


def on_device(points, rank, counts, w_qkv_one, w_out_one, w_up, w_down, w_qkv_two, w_out_two):
    owner_count = lax.axis_size("win")
    group_count = lax.axis_size("grp")
    win_index = lax.axis_index("win")
    grp_index = lax.axis_index("grp")
    local_points = points.shape[2]
    model_dim = points.shape[3]
    blocks = counts.shape[2]
    slots_all = blocks * WINDOW_SLOTS
    capacity = 2 * local_points // owner_count
    buffer_rows = owner_count * capacity
    dilation_stride = WINDOW_SLOTS // group_count
    rows_x = points.reshape(local_points, model_dim)
    point_rank = rank.reshape(local_points)
    column_counts = lax.dynamic_index_in_dim(counts, grp_index, 0, keepdims=False)

    owner_dev = lax.div(point_rank, local_points)
    owner_ids = jnp.arange(owner_count, dtype=jnp.int32)
    choose = (owner_dev[:, None] == owner_ids[None, :]).astype(jnp.int32)
    point_ids = jnp.arange(local_points, dtype=jnp.int32)
    lower = (point_ids[None, :] <= point_ids[:, None]).astype(jnp.bfloat16)
    running = jnp.dot(lower, choose.astype(jnp.bfloat16), preferred_element_type=jnp.float32)
    peer_order = jnp.sum(choose * (running.astype(jnp.int32) - 1), axis=1)
    send_place = owner_dev * capacity + peer_order
    buffer_ids = jnp.arange(buffer_rows, dtype=jnp.int32)
    send_hot = (buffer_ids[:, None] == send_place[None, :]).astype(jnp.bfloat16)

    window_ends = jnp.cumsum(column_counts, axis=1)
    starts = window_ends - column_counts
    offset = lax.rem(point_rank, local_points)
    table = jnp.concatenate(
        [lax.div(window_ends, SLOT_BASE), lax.rem(window_ends, SLOT_BASE), lax.div(starts, SLOT_BASE), lax.rem(starts, SLOT_BASE)], axis=1
    ).astype(jnp.bfloat16)
    picked = jnp.dot(choose.astype(jnp.bfloat16), table, preferred_element_type=jnp.float32)
    picked = picked.astype(jnp.int32)
    owner_ends = picked[:, :blocks] * SLOT_BASE + picked[:, blocks : 2 * blocks]
    owner_starts = picked[:, 2 * blocks : 3 * blocks] * SLOT_BASE + picked[:, 3 * blocks :]
    window = jnp.sum((owner_ends <= offset[:, None]).astype(jnp.int32), axis=1)
    block_ids = jnp.arange(blocks, dtype=jnp.int32)
    block_pick = (window[:, None] == block_ids[None, :]).astype(jnp.int32)
    dest_slot = window * WINDOW_SLOTS + offset - jnp.sum(block_pick * owner_starts, axis=1)
    slot_code = dest_slot + 1
    tail_ids = jnp.arange(TAIL, dtype=jnp.int32)
    code_cols = jnp.where(
        tail_ids[None, :] == 0,
        lax.div(slot_code, SLOT_BASE)[:, None],
        jnp.where(tail_ids[None, :] == 1, lax.rem(slot_code, SLOT_BASE)[:, None], 0),
    ).astype(jnp.bfloat16)
    outgoing = place(send_hot, jnp.concatenate([rows_x, code_cols], axis=1))
    receiving = lax.all_to_all(
        outgoing.reshape(owner_count, capacity, model_dim + TAIL),
        "win",
        split_axis=0,
        concat_axis=0,
        tiled=True,
    ).reshape(buffer_rows, model_dim + TAIL)
    arrived = receiving[:, :model_dim]
    code_back = receiving[:, model_dim:].astype(jnp.int32)
    arrived_slot = code_back[:, 0] * SLOT_BASE + code_back[:, 1] - 1
    own_counts = lax.dynamic_index_in_dim(column_counts, win_index, 0, keepdims=False)
    slot_ids = jnp.arange(slots_all, dtype=jnp.int32)
    recv_hot = (slot_ids[:, None] == arrived_slot.reshape(1, buffer_rows)).astype(jnp.bfloat16)
    padded_x = place(recv_hot, arrived)

    column = jnp.arange(WINDOW_SLOTS, dtype=jnp.int32)
    usable_mask = column[None, :] < own_counts[:, None]
    first_pad = feed_forward(attention_block(padded_x, usable_mask, w_qkv_one, w_out_one), w_up, w_down)
    dilated_rows = lax.all_to_all(
        first_pad.reshape(blocks, dilation_stride, group_count, model_dim),
        "grp",
        split_axis=2,
        concat_axis=1,
        tiled=True,
    )
    owner_counts = lax.dynamic_index_in_dim(counts, win_index, 1, keepdims=False)
    k_ids = jnp.arange(dilation_stride, dtype=jnp.int32)
    valid_marks = (k_ids[None, None, :] * group_count + grp_index) < jnp.transpose(owner_counts)[
        :, :, None
    ]
    block_count = dilated_rows.shape[0]
    flat_rows = dilated_rows.reshape(block_count * WINDOW_SLOTS, model_dim)
    mixed_rows = attention_block(
        flat_rows, valid_marks.reshape(block_count, WINDOW_SLOTS), w_qkv_two, w_out_two
    ).reshape(
        block_count, WINDOW_SLOTS, 1, model_dim
    )
    second_pad = lax.all_to_all(mixed_rows, "grp", split_axis=1, concat_axis=2, tiled=True).reshape(
        slots_all, model_dim
    )
    returning = place_back(recv_hot, second_pad)
    returned = lax.all_to_all(returning, "win", split_axis=0, concat_axis=0, tiled=True)
    encoded = place_back(send_hot, returned)
    return encoded.reshape(1, 1, local_points, model_dim)


def solution(mesh):
    return jax.shard_map(
        on_device,
        mesh=mesh,
        in_specs=(
            P("win", "grp", None, None),
            P("win", "grp", None),
            P(),
            P(),
            P(),
            P(),
            P(),
            P(),
            P(),
        ),
        out_specs=P("win", "grp", None, None),
        check_vma=False,
    )
```

```python
import jax
import jax.numpy as jnp
from jax import lax
from jax.sharding import PartitionSpec as P

HEAD_DIM = 32
WINDOW_SLOTS = 128


EPSILON = 1e-05
MASKED = -1e30
SLOT_BASE = 32
TAIL = 128


def normalize(row_data):
    values = row_data.astype(jnp.float32)
    center = values - jnp.mean(values, axis=-1, keepdims=True)
    spread = jnp.mean(center * center, axis=-1, keepdims=True)
    return (center * lax.rsqrt(spread + EPSILON)).astype(jnp.bfloat16)


def project(row_data, weight):
    return jnp.dot(normalize(row_data), weight, preferred_element_type=jnp.float32).astype(
        jnp.bfloat16
    )


def attention_block(row_data, valid, w_qkv, w_out):
    rows_count, model_dim = row_data.shape
    heads_count = model_dim // HEAD_DIM
    block_count = rows_count // WINDOW_SLOTS
    normed = normalize(row_data)
    w_split = w_qkv.reshape(model_dim, 3, heads_count, HEAD_DIM)

    def head_major(part):
        out = jnp.einsum("nd,dhe->hne", normed, w_split[:, part], preferred_element_type=jnp.float32)
        return out.astype(jnp.bfloat16).reshape(heads_count, block_count, WINDOW_SLOTS, HEAD_DIM)

    query, key, value = head_major(0), head_major(1), head_major(2)
    scores = jnp.einsum(
        "hbqe,hbke->hbqk", query, key, preferred_element_type=jnp.float32
    ) * HEAD_DIM ** (-0.5)
    scores = jnp.where(valid[None, :, None, :], scores, MASKED)
    row_max = jnp.max(scores, axis=-1, keepdims=True)
    weights = jnp.exp(scores - row_max)
    weights = (weights / jnp.sum(weights, axis=-1, keepdims=True)).astype(jnp.bfloat16)
    context = jnp.einsum("hbqk,hbke->hbqe", weights, value, preferred_element_type=jnp.float32)
    context = context.astype(jnp.bfloat16).reshape(heads_count, rows_count, HEAD_DIM)
    mixed = jnp.einsum(
        "hne,hed->nd",
        context,
        w_out.reshape(heads_count, HEAD_DIM, model_dim),
        preferred_element_type=jnp.float32,
    )
    return (row_data.astype(jnp.float32) + mixed).astype(jnp.bfloat16)


def feed_forward(row_data, w_up, w_down):
    hidden = jax.nn.gelu(
        jnp.dot(normalize(row_data), w_up, preferred_element_type=jnp.float32), approximate=True
    ).astype(jnp.bfloat16)
    return (
        row_data.astype(jnp.float32) + jnp.dot(hidden, w_down, preferred_element_type=jnp.float32)
    ).astype(jnp.bfloat16)


def place(onehot, rows):
    return jnp.dot(onehot, rows, preferred_element_type=jnp.float32).astype(jnp.bfloat16)


def place_back(onehot, rows):
    return lax.dot_general(
        onehot, rows, (((0,), (0,)), ((), ())), preferred_element_type=jnp.float32
    ).astype(jnp.bfloat16)


def on_device(points, rank, counts, w_qkv_one, w_out_one, w_up, w_down, w_qkv_two, w_out_two):
    owner_count = lax.axis_size("win")
    group_count = lax.axis_size("grp")
    win_index = lax.axis_index("win")
    grp_index = lax.axis_index("grp")
    local_points = points.shape[2]
    model_dim = points.shape[3]
    blocks = counts.shape[2]
    slots_all = blocks * WINDOW_SLOTS
    capacity = 2 * local_points // owner_count
    buffer_rows = owner_count * capacity
    dilation_stride = WINDOW_SLOTS // group_count
    rows_x = points.reshape(local_points, model_dim)
    point_rank = rank.reshape(local_points)
    column_counts = lax.dynamic_index_in_dim(counts, grp_index, 0, keepdims=False)

    owner_dev = point_rank // local_points
    owner_ids = jnp.arange(owner_count, dtype=jnp.int32)
    choose = (owner_dev[:, None] == owner_ids[None, :]).astype(jnp.int32)
    point_ids = jnp.arange(local_points, dtype=jnp.int32)
    lower = (point_ids[None, :] <= point_ids[:, None]).astype(jnp.bfloat16)
    running = jnp.dot(lower, choose.astype(jnp.bfloat16), preferred_element_type=jnp.float32)
    peer_order = jnp.sum(choose * (running.astype(jnp.int32) - 1), axis=1)
    send_place = owner_dev * capacity + peer_order
    buffer_ids = jnp.arange(buffer_rows, dtype=jnp.int32)
    send_hot = (send_place[:, None] == buffer_ids[None, :]).astype(jnp.bfloat16)

    window_ends = jnp.cumsum(column_counts, axis=1)
    starts = window_ends - column_counts
    offset = point_rank % local_points
    table = jnp.concatenate(
        [window_ends // SLOT_BASE, window_ends % SLOT_BASE, starts // SLOT_BASE, starts % SLOT_BASE], axis=1
    ).astype(jnp.bfloat16)
    picked = jnp.dot(choose.astype(jnp.bfloat16), table, preferred_element_type=jnp.float32)
    picked = picked.astype(jnp.int32)
    owner_ends = picked[:, :blocks] * SLOT_BASE + picked[:, blocks : 2 * blocks]
    owner_starts = picked[:, 2 * blocks : 3 * blocks] * SLOT_BASE + picked[:, 3 * blocks :]
    window = jnp.sum((owner_ends <= offset[:, None]).astype(jnp.int32), axis=1)
    block_ids = jnp.arange(blocks, dtype=jnp.int32)
    block_pick = (window[:, None] == block_ids[None, :]).astype(jnp.int32)
    dest_slot = window * WINDOW_SLOTS + offset - jnp.sum(block_pick * owner_starts, axis=1)
    slot_code = dest_slot + 1
    tail_ids = jnp.arange(TAIL, dtype=jnp.int32)
    code_cols = jnp.where(
        tail_ids[None, :] == 0,
        (slot_code // SLOT_BASE)[:, None],
        jnp.where(tail_ids[None, :] == 1, (slot_code % SLOT_BASE)[:, None], 0),
    ).astype(jnp.bfloat16)
    outgoing = place_back(send_hot, jnp.concatenate([rows_x, code_cols], axis=1))
    receiving = lax.all_to_all(
        outgoing.reshape(owner_count, capacity, model_dim + TAIL),
        "win",
        split_axis=0,
        concat_axis=0,
        tiled=True,
    ).reshape(buffer_rows, model_dim + TAIL)
    arrived = receiving[:, :model_dim]
    code_back = receiving[:, model_dim:].astype(jnp.int32)
    arrived_slot = code_back[:, 0] * SLOT_BASE + code_back[:, 1] - 1
    own_counts = lax.dynamic_index_in_dim(column_counts, win_index, 0, keepdims=False)
    slot_ids = jnp.arange(slots_all, dtype=jnp.int32)
    recv_hot = (slot_ids[:, None] == arrived_slot.reshape(1, buffer_rows)).astype(jnp.bfloat16)
    padded_x = place(recv_hot, arrived)

    column = jnp.arange(WINDOW_SLOTS, dtype=jnp.int32)
    usable_mask = column[None, :] < own_counts[:, None]
    first_pad = feed_forward(attention_block(padded_x, usable_mask, w_qkv_one, w_out_one), w_up, w_down)
    dilated_rows = lax.all_to_all(
        first_pad.reshape(blocks, dilation_stride, group_count, model_dim),
        "grp",
        split_axis=2,
        concat_axis=1,
        tiled=True,
    )
    owner_counts = lax.dynamic_index_in_dim(counts, win_index, 1, keepdims=False)
    k_ids = jnp.arange(dilation_stride, dtype=jnp.int32)
    valid_marks = (k_ids[None, None, :] * group_count + grp_index) < jnp.transpose(owner_counts)[
        :, :, None
    ]
    block_count = dilated_rows.shape[0]
    flat_rows = dilated_rows.reshape(block_count * WINDOW_SLOTS, model_dim)
    mixed_rows = attention_block(
        flat_rows, valid_marks.reshape(block_count, WINDOW_SLOTS), w_qkv_two, w_out_two
    ).reshape(
        block_count, WINDOW_SLOTS, 1, model_dim
    )
    second_pad = lax.all_to_all(mixed_rows, "grp", split_axis=1, concat_axis=2, tiled=True).reshape(
        slots_all, model_dim
    )
    returning = place_back(recv_hot, second_pad)
    returned = lax.all_to_all(returning, "win", split_axis=0, concat_axis=0, tiled=True)
    encoded = place(send_hot, returned)
    return encoded.reshape(1, 1, local_points, model_dim)


def solution(mesh):
    return jax.shard_map(
        on_device,
        mesh=mesh,
        in_specs=(
            P("win", "grp", None, None),
            P("win", "grp", None),
            P(),
            P(),
            P(),
            P(),
            P(),
            P(),
            P(),
        ),
        out_specs=P("win", "grp", None, None),
        check_vma=False,
    )
```
